128 devices in a mesh: req: 4 (over x_lo, core), kv: 32 (over z, x_hi, y).
Axes of the slice: x: 4 (x_hi: 2, x_lo: 2; x = x_hi * 2 + x_lo), y: 4, z: 4, core: 2. Of those that a mesh axis runs over, the one named last changes fastest.
Arguments:
- hidden_in: bfloat16 [2048, 4096], P('req'), may hold values from -6 to 6
- ln_gains: float32 [2, 4096], replicated, may hold values from 0.1 to 1.9
- qkv_weight: bfloat16 [4096, 3, 4096], P('req', None, 'kv'), may hold values from -0.09375 to 0.09375
- dense_weight: bfloat16 [4096, 4096], P('kv', 'req'), may hold values from -0.09375 to 0.09375
- up_weight: bfloat16 [4096, 16384], P('req', 'kv'), may hold values from -0.09375 to 0.09375
- down_weight: bfloat16 [16384, 4096], P('kv', 'req'), may hold values from -0.046875 to 0.046875
- cache: bfloat16 [4, 256, 2, 32, 128, 128], P('req', 'kv'), may hold values from -200 to 200
- cached_len: int32 [8], P('req'), may hold values from 1 to 16384, as said below
- page_table: int32 [8, 128], P('req'), may hold values from 0 to 255, as said below
Outputs:
- hidden_out: float32 [2048, 4096], P('req', 'kv')
The draws below stay inside these ranges and needn't reach their ends.
Inputs may be any that keep to these rules, and one draw needn't show every extreme that they name: `page_table`: within each group of 2 consecutive requests the entries are distinct and together name each of the group's 256 slots once. `cached_len`: some request has exactly 16384 cached tokens.
All inputs are finite; a program needn't handle non-finite values.
Results may differ from the reference program's by a relative error of at most 0.012.
The reference program's roundings to bfloat16 on the way count: a program that leaves them out, or rounds other values in their place, can miss the bound.
Values may be sent and summed in bfloat16 or wider, within the bound.
No kernel may reach another device: no remote copies, remote signals or barrier semaphores. Data moves between devices by JAX's collectives and lax.ppermute only.
A program may use at most 192 MiB of HBM per device.

```python
import jax
import jax.numpy as jnp
from jax import lax

D = 4096
HEADS = 32
HD = 128
ROT = 32
FF = 16384
REQ_GRP = 2
SPAN = 256
PAGE = 128
GROUPS = 4
REQS = 8
SLOTS = 256
MAXP = 128
MAXLEN = 16384
TOKENS = 2048


def draw_cache(key, part):
    values = jax.random.normal(key, (GROUPS, SLOTS, 2, HEADS, PAGE, HD), jnp.float32)
    return jnp.clip(values, -200.0, 200.0).astype(jnp.bfloat16)


def draw_cached_len(key, part):
    base = jax.random.randint(key, (REQS,), 1, MAXLEN + 1, jnp.int32)
    pick = jax.random.randint(jax.random.fold_in(key, 1), (), 0, REQS, jnp.int32)
    return base.at[pick].set(MAXLEN)


def draw_page_table(key, part):
    keys = jax.random.split(key, GROUPS)
    perms = jax.vmap(lambda k: jax.random.permutation(k, SLOTS))(keys)
    return perms.reshape(REQS, MAXP).astype(jnp.int32)


def block_levels(key, extent, pieces, low, top_value):
    level = 1.0
    for dim, parts in pieces:
        heights = jax.random.uniform(jax.random.fold_in(jax.random.fold_in(key, 6), dim), (parts,), jnp.float32, low / len(pieces), top_value / len(pieces))
        level = level * jnp.repeat(jnp.exp(heights), extent[dim] // parts).reshape((-1,) + (1,) * (len(extent) - 1 - dim))
    return level


def bell_draw(key, shape, scale, reach, shards=(), held_as=jnp.bfloat16):
    factor_of = block_levels(key, shape, shards, -0.22, 0.18) if shards else 1.0
    array = jax.random.normal(key, shape, jnp.float32) * scale * factor_of
    return jnp.minimum(jnp.maximum(array, -reach), reach).astype(held_as)


def setup_inputs(seed: int = 0) -> dict:
    arg_keys = jax.random.split(jax.random.key(seed), 10)
    hidden_in = bell_draw(arg_keys[0], (TOKENS, D), 1.0, 6.0, ((0, 4),))
    ln_gains = jnp.clip(1.0 + 0.18 * jax.random.normal(arg_keys[1], (2, D), jnp.float32), 0.1, 1.9)
    qkv_weight = bell_draw(arg_keys[2], (D, 3, D), D ** -0.5, 0.09375, ((0, 4), (2, 32)))
    dense_weight = bell_draw(arg_keys[3], (D, D), D ** -0.5, 0.09375, ((0, 32), (1, 4)))
    up_weight = bell_draw(arg_keys[4], (D, FF), D ** -0.5, 0.09375, ((0, 4), (1, 32)))
    down_weight = bell_draw(arg_keys[5], (FF, D), FF ** -0.5, 0.046875, ((0, 32), (1, 4)))
    cache = draw_cache(jax.random.fold_in(arg_keys[9], 71), 0)
    cached_len = draw_cached_len(jax.random.fold_in(arg_keys[9], 71), 0)
    page_table = draw_page_table(jax.random.fold_in(arg_keys[9], 71), 0)
    return {"hidden_in": hidden_in, "ln_gains": ln_gains, "qkv_weight": qkv_weight, "dense_weight": dense_weight, "up_weight": up_weight, "down_weight": down_weight, "cache": cache, "cached_len": cached_len, "page_table": page_table}


def layer_norm(x, gain):
    mean = lax.optimization_barrier(jnp.mean(x, axis=-1, keepdims=True))
    cent = x - mean
    var = lax.optimization_barrier(jnp.mean(cent * cent, axis=-1, keepdims=True))
    return cent * jax.lax.rsqrt(var + 1e-05) * gain

def rotate(t, pos):
    half = ROT // 2
    freq = 10000.0 ** (-(jnp.arange(half, dtype=jnp.float32) * 2.0 / ROT))
    angle = pos[:, None] * freq[None, :]
    cosine = jnp.cos(angle)[:, None, :]
    sine = jnp.sin(angle)[:, None, :]
    first = t[..., :half]
    second = t[..., half:ROT]
    return jnp.concatenate([first * cosine - second * sine, second * cosine + first * sine, t[..., ROT:]], axis=-1)

def reference(hidden_in, ln_gains, qkv_weight, dense_weight, up_weight, down_weight, cache, cached_len, page_table):
    x = hidden_in.astype(jnp.float32)
    h1 = layer_norm(x, ln_gains[0]).astype(jnp.bfloat16)
    h2 = layer_norm(x, ln_gains[1]).astype(jnp.bfloat16)
    qkv = jnp.dot(h1, qkv_weight.reshape(D, 3 * D), preferred_element_type=jnp.float32).reshape(TOKENS, 3, HEADS, HD)
    offsets = jnp.arange(SPAN, dtype=jnp.int32)
    pos = (cached_len[:, None] + offsets[None, :]).reshape(TOKENS).astype(jnp.float32)
    query = rotate(qkv[:, 0], pos).astype(jnp.bfloat16)
    key = rotate(qkv[:, 1], pos).astype(jnp.bfloat16)
    value = qkv[:, 2].astype(jnp.bfloat16)
    scale = 1.0 / HD ** 0.5
    causal = offsets[None, :] <= offsets[:, None]
    outputs = []
    for req in range(REQS):
        group = req // REQ_GRP
        q_req = query[req * SPAN:(req + 1) * SPAN].astype(jnp.float32)
        k_req = key[req * SPAN:(req + 1) * SPAN].astype(jnp.float32)
        v_req = value[req * SPAN:(req + 1) * SPAN].astype(jnp.float32)
        pages = cache[group][page_table[req]]
        k_old = jnp.transpose(pages[:, 0], (1, 0, 2, 3)).reshape(HEADS, MAXLEN, HD).astype(jnp.float32)
        v_old = jnp.transpose(pages[:, 1], (1, 0, 2, 3)).reshape(HEADS, MAXLEN, HD).astype(jnp.float32)
        live = jnp.arange(MAXLEN, dtype=jnp.int32) < cached_len[req]
        s_old = jnp.einsum('qhd,hkd->hqk', q_req, k_old) * scale
        s_new = jnp.einsum('qhd,khd->hqk', q_req, k_req) * scale
        s_old = jnp.where(live[None, None, :], s_old, -1e+30)
        s_new = jnp.where(causal[None], s_new, -1e+30)
        top = jnp.maximum(lax.optimization_barrier(jnp.max(s_old, axis=-1)), lax.optimization_barrier(jnp.max(s_new, axis=-1)))
        p_old = jnp.where(live[None, None, :], jnp.exp(s_old - top[..., None]), 0.0).astype(jnp.bfloat16).astype(jnp.float32)
        p_new = jnp.where(causal[None], jnp.exp(s_new - top[..., None]), 0.0).astype(jnp.bfloat16).astype(jnp.float32)
        numer = jnp.einsum('hqk,hkd->hqd', p_old, v_old) + jnp.einsum('hqk,khd->hqd', p_new, v_req)
        denom = lax.optimization_barrier(jnp.sum(p_old, axis=-1)) + lax.optimization_barrier(jnp.sum(p_new, axis=-1))
        att = numer / denom[..., None]
        outputs.append(jnp.transpose(att, (1, 0, 2)).reshape(SPAN, D))
    attn = jnp.concatenate(outputs, axis=0).astype(jnp.bfloat16)
    branch = jnp.dot(attn, dense_weight, preferred_element_type=jnp.float32)
    hidden = jax.nn.gelu(jnp.dot(h2, up_weight, preferred_element_type=jnp.float32), approximate=False).astype(jnp.bfloat16)
    mlp = jnp.dot(hidden, down_weight, preferred_element_type=jnp.float32)
    return x + branch + mlp
```

```python
import jax
import jax.numpy as jnp
from jax import lax
from jax.sharding import PartitionSpec as P

D = 4096
HEADS = 32
HD = 128
ROT = 32
PAGE = 128


def layer_norm(x, gain):
    mean = jnp.mean(x, axis=-1, keepdims=True)
    cent = x - mean
    var = jnp.mean(cent * cent, axis=-1, keepdims=True)
    return cent * lax.rsqrt(var + 1e-05) * gain


def rotate(t, pos):
    half = ROT // 2
    freq = 10000.0 ** (-(jnp.arange(half, dtype=jnp.float32) * 2.0 / ROT))
    angle = pos[:, None] * freq[None, :]
    cosine = jnp.cos(angle)[:, None, :]
    sine = jnp.sin(angle)[:, None, :]
    first = t[..., :half]
    second = t[..., half:ROT]
    return jnp.concatenate(
        [first * cosine - second * sine, second * cosine + first * sine, t[..., ROT:]], axis=-1
    )


def online_update(state, scores, live, values):
    top, total, accum = state
    masked = jnp.where(live, scores, -1e30)
    new_top = jnp.maximum(top, jnp.max(masked, axis=-1))
    weights = jnp.where(live, jnp.exp(scores - new_top[..., None]), 0.0).astype(jnp.bfloat16)
    factor = jnp.exp(top - new_top)
    total = total * factor + jnp.sum(weights.astype(jnp.float32), axis=-1)
    accum = accum * factor[..., None] + jnp.einsum(
        "hqk,hkd->hqd", weights, values, preferred_element_type=jnp.float32
    )
    return (new_top, total, accum)


def per_device(
    hidden_in,
    ln_gains,
    qkv_weight,
    dense_weight,
    up_weight,
    down_weight,
    cache,
    cached_len,
    page_table,
):
    n_kv = lax.axis_size("kv")
    me_kv = lax.axis_index("kv")
    rows = hidden_in.shape[0]
    groups_here = cached_len.shape[0]
    span_rows = rows // groups_here
    width_loc = qkv_weight.shape[2]
    heads_loc = width_loc // HD
    scale = 1.0 / HD**0.5
    x = hidden_in.astype(jnp.float32)
    h1 = layer_norm(x, ln_gains[0]).astype(jnp.bfloat16)
    h2 = layer_norm(x, ln_gains[1]).astype(jnp.bfloat16)
    qkv_piece = lax.all_gather(qkv_weight, "req", axis=0, tiled=True)
    up_piece = lax.all_gather(up_weight, "req", axis=0, tiled=True)
    count = qkv_piece.shape[0]
    qkv_acc = jnp.dot(
        h1, qkv_piece.reshape(count, 3 * width_loc), preferred_element_type=jnp.float32
    )
    up_acc = jnp.dot(h2, up_piece, preferred_element_type=jnp.float32)
    qkv = qkv_acc
    qkv = qkv.reshape(rows, 3, heads_loc, HD)
    offsets = jnp.arange(span_rows, dtype=jnp.int32)
    pos = (cached_len[:, None] + offsets[None, :]).reshape(rows).astype(jnp.float32)
    query = rotate(qkv[:, 0], pos).astype(jnp.bfloat16)
    key_new = rotate(qkv[:, 1], pos).astype(jnp.bfloat16)
    value_new = qkv[:, 2].astype(jnp.bfloat16)
    q_grp = query.reshape(groups_here, span_rows, heads_loc, HD)
    k_grp = key_new.reshape(groups_here, span_rows, heads_loc, HD)
    v_grp = value_new.reshape(groups_here, span_rows, heads_loc, HD)
    causal = offsets[None, :] <= offsets[:, None]
    s_new = jnp.einsum("gqhd,gkhd->ghqk", q_grp, k_grp, preferred_element_type=jnp.float32) * scale
    s_new = jnp.where(causal[None, None], s_new, -1e30)
    top_new = jnp.max(s_new, axis=-1)
    p_new = jnp.where(causal[None, None], jnp.exp(s_new - top_new[..., None]), 0.0).astype(
        jnp.bfloat16
    )
    total_new = jnp.sum(p_new.astype(jnp.float32), axis=-1)
    accum_new = jnp.einsum("ghqk,gkhd->ghqd", p_new, v_grp, preferred_element_type=jnp.float32)
    q_all = lax.all_gather(query.reshape(rows, width_loc), "kv", axis=1, tiled=True)
    q_all = q_all.reshape(groups_here, span_rows, HEADS, HD)
    local_cache = cache[0]
    slots_here = local_cache.shape[0]
    slot_ids = me_kv * slots_here + jnp.arange(slots_here, dtype=jnp.int32)
    match = (page_table[None, :, :] == slot_ids[:, None, None]).astype(jnp.int32)
    owner_req = jnp.sum(
        match * jnp.arange(groups_here, dtype=jnp.int32)[None, :, None], axis=(1, 2)
    )
    owner_page = jnp.sum(
        match * jnp.arange(page_table.shape[1], dtype=jnp.int32)[None, None, :], axis=(1, 2)
    )
    page_pos = jnp.arange(PAGE, dtype=jnp.int32)

    def visit(slot, state):
        tops, totals, accums = state
        req = owner_req[slot]
        page_kv = lax.dynamic_index_in_dim(local_cache, slot, 0, keepdims=False)
        q_req = lax.dynamic_index_in_dim(q_all, req, 0, keepdims=False)
        scores = (
            jnp.einsum("qhd,hkd->hqk", q_req, page_kv[0], preferred_element_type=jnp.float32)
            * scale
        )
        length = lax.dynamic_index_in_dim(cached_len, req, 0, keepdims=False)
        live = (owner_page[slot] * PAGE + page_pos < length)[None, None, :]
        part_state = (
            lax.dynamic_index_in_dim(tops, req, 0, keepdims=False),
            lax.dynamic_index_in_dim(totals, req, 0, keepdims=False),
            lax.dynamic_index_in_dim(accums, req, 0, keepdims=False),
        )
        top, total, accum = online_update(part_state, scores, live, page_kv[1])
        tops = lax.dynamic_update_index_in_dim(tops, top, req, 0)
        totals = lax.dynamic_update_index_in_dim(totals, total, req, 0)
        accums = lax.dynamic_update_index_in_dim(accums, accum, req, 0)
        return (tops, totals, accums)

    empty = (
        jnp.full((groups_here, HEADS, span_rows), -1e30, jnp.float32),
        jnp.zeros((groups_here, HEADS, span_rows), jnp.float32),
        jnp.zeros((groups_here, HEADS, span_rows, HD), jnp.float32),
    )
    tops, totals, accums = lax.fori_loop(0, slots_here, visit, empty)
    own = lax.dynamic_slice_in_dim(tops, me_kv * heads_loc, heads_loc, 1)
    with_new = lax.dynamic_update_slice_in_dim(
        tops, jnp.maximum(own, top_new), me_kv * heads_loc, 1
    )
    largest = jnp.max(lax.all_gather(with_new, "kv", axis=0, tiled=False), axis=0)
    factor = jnp.exp(tops - largest)
    tot_rows = (totals * factor).reshape(groups_here, HEADS, span_rows // HD, HD)
    packed = jnp.concatenate([accums * factor[..., None], tot_rows], axis=2)
    summed = lax.psum_scatter(packed, "kv", scatter_dimension=1, tiled=True)
    sum_acc = summed[:, :, :span_rows]
    sum_tot = summed[:, :, span_rows:].reshape(groups_here, heads_loc, span_rows)
    own_largest = lax.dynamic_slice_in_dim(largest, me_kv * heads_loc, heads_loc, 1)
    fresh = jnp.exp(top_new - own_largest)
    numer = sum_acc + accum_new * fresh[..., None]
    denom = sum_tot + total_new * fresh
    att = (numer / denom[..., None]).astype(jnp.bfloat16)
    att = jnp.transpose(att, (0, 2, 1, 3)).reshape(rows, width_loc)
    hidden = jax.nn.gelu(up_acc, approximate=False).astype(jnp.bfloat16)
    dense_piece = lax.all_gather(dense_weight, "req", axis=1, tiled=True)
    down_piece = lax.all_gather(down_weight, "req", axis=1, tiled=True)
    value = jnp.dot(att, dense_piece, preferred_element_type=jnp.float32) + jnp.dot(
        hidden, down_piece, preferred_element_type=jnp.float32
    )
    summed = lax.psum_scatter(value, "kv", scatter_dimension=1, tiled=True)
    width_out = D // n_kv
    residual = lax.dynamic_slice_in_dim(x, me_kv * width_out, width_out, 1)
    return residual + summed


def solution(mesh):
    placed = (
        P("req", None),
        P(),
        P("req", None, "kv"),
        P("kv", "req"),
        P("req", "kv"),
        P("kv", "req"),
        P("req", "kv", None, None, None, None),
        P("req"),
        P("req", None),
    )
    return jax.shard_map(
        per_device, mesh=mesh, in_specs=placed, out_specs=P("req", "kv"), check_vma=False
    )
```

```python
import jax
import jax.numpy as jnp
from jax import lax
from jax.sharding import PartitionSpec as P
from jax.experimental import pallas as pl

D = 4096
HEADS = 32
HD = 128
ROT = 32
PAGE = 128


def layer_norm(x, gain):
    mean = jnp.mean(x, axis=-1, keepdims=True)
    cent = x - mean
    var = jnp.mean(cent * cent, axis=-1, keepdims=True)
    return cent * lax.rsqrt(var + 1e-05) * gain


def rotate(t, pos):
    half = ROT // 2
    freq = 10000.0 ** (-(jnp.arange(half, dtype=jnp.float32) * 2.0 / ROT))
    angle = pos[:, None] * freq[None, :]
    cosine = jnp.cos(angle)[:, None, :]
    sine = jnp.sin(angle)[:, None, :]
    first = t[..., :half]
    second = t[..., half:ROT]
    return jnp.concatenate(
        [first * cosine - second * sine, second * cosine + first * sine, t[..., ROT:]], axis=-1
    )


def attend_kernel(q_ref, k_ref, v_ref, live_ref, acc_ref, top_ref, tot_ref):
    scale = 1.0 / HD**0.5
    slots = k_ref.shape[0]
    q = q_ref[...]
    k = k_ref[...].reshape(slots * PAGE, HD)
    v = v_ref[...].reshape(slots * PAGE, HD)
    scores = (
        lax.dot_general(q, k, (((1,), (1,)), ((), ())), preferred_element_type=jnp.float32)
        * scale
    )
    live = live_ref[...] > 0
    top = jnp.max(jnp.where(live, scores, -1e30), axis=1, keepdims=True)
    weights = jnp.where(live, jnp.exp(scores - top), 0.0).astype(jnp.bfloat16)
    tot_ref[...] = jnp.sum(weights.astype(jnp.float32), axis=1, keepdims=True)
    top_ref[...] = top
    acc_ref[...] = jnp.dot(weights, v, preferred_element_type=jnp.float32)


def attend_pages(q_all, local_cache, live):
    groups, span = live.shape[0], q_all.shape[0] // live.shape[0]
    slots = local_cache.shape[0]
    heads = local_cache.shape[2]
    page_spec = lambda kv: pl.BlockSpec(
        (slots, None, None, PAGE, HD), lambda g, h: (0, kv, h, 0, 0)
    )
    return pl.pallas_call(
        attend_kernel,
        grid=(groups, heads),
        in_specs=[
            pl.BlockSpec((span, HD), lambda g, h: (g, h)),
            page_spec(0),
            page_spec(1),
            pl.BlockSpec((None, 1, slots * PAGE), lambda g, h: (g, 0, 0)),
        ],
        out_specs=[
            pl.BlockSpec((None, None, span, HD), lambda g, h: (h, g, 0, 0)),
            pl.BlockSpec((None, None, span, 1), lambda g, h: (h, g, 0, 0)),
            pl.BlockSpec((None, None, span, 1), lambda g, h: (h, g, 0, 0)),
        ],
        out_shape=[
            jax.ShapeDtypeStruct((heads, groups, span, HD), jnp.float32),
            jax.ShapeDtypeStruct((heads, groups, span, 1), jnp.float32),
            jax.ShapeDtypeStruct((heads, groups, span, 1), jnp.float32),
        ],
        cost_estimate=pl.CostEstimate(
            flops=4 * groups * heads * span * slots * PAGE * HD,
            transcendentals=groups * heads * span * slots * PAGE,
            bytes_accessed=groups * local_cache.size * 2 + q_all.size * 2
            + groups * heads * span * HD * 4,
        ),
    )(q_all, local_cache, local_cache, live)


def per_device(
    hidden_in,
    ln_gains,
    qkv_weight,
    dense_weight,
    up_weight,
    down_weight,
    cache,
    cached_len,
    page_table,
):
    n_kv = lax.axis_size("kv")
    me_kv = lax.axis_index("kv")
    rows = hidden_in.shape[0]
    groups_here = cached_len.shape[0]
    span_rows = rows // groups_here
    width_loc = qkv_weight.shape[2]
    heads_loc = width_loc // HD
    scale = 1.0 / HD**0.5
    x = hidden_in.astype(jnp.float32)
    h1 = layer_norm(x, ln_gains[0]).astype(jnp.bfloat16)
    h2 = layer_norm(x, ln_gains[1]).astype(jnp.bfloat16)
    qkv_piece = lax.all_gather(qkv_weight, "req", axis=0, tiled=True)
    up_piece = lax.all_gather(up_weight, "req", axis=0, tiled=True)
    count = qkv_piece.shape[0]
    qkv_acc = jnp.dot(
        h1, qkv_piece.reshape(count, 3 * width_loc), preferred_element_type=jnp.float32
    )
    up_acc = jnp.dot(h2, up_piece, preferred_element_type=jnp.float32)
    qkv = qkv_acc
    qkv = qkv.reshape(rows, 3, heads_loc, HD)
    offsets = jnp.arange(span_rows, dtype=jnp.int32)
    pos = (cached_len[:, None] + offsets[None, :]).reshape(rows).astype(jnp.float32)
    query = rotate(qkv[:, 0], pos).astype(jnp.bfloat16)
    key_new = rotate(qkv[:, 1], pos).astype(jnp.bfloat16)
    value_new = qkv[:, 2].astype(jnp.bfloat16)
    q_grp = query.reshape(groups_here, span_rows, heads_loc, HD)
    k_grp = key_new.reshape(groups_here, span_rows, heads_loc, HD)
    v_grp = value_new.reshape(groups_here, span_rows, heads_loc, HD)
    causal = offsets[None, :] <= offsets[:, None]
    s_new = jnp.einsum("gqhd,gkhd->ghqk", q_grp, k_grp, preferred_element_type=jnp.float32) * scale
    s_new = jnp.where(causal[None, None], s_new, -1e30)
    top_new = jnp.max(s_new, axis=-1)
    p_new = jnp.where(causal[None, None], jnp.exp(s_new - top_new[..., None]), 0.0).astype(
        jnp.bfloat16
    )
    total_new = jnp.sum(p_new.astype(jnp.float32), axis=-1)
    accum_new = jnp.einsum("ghqk,gkhd->ghqd", p_new, v_grp, preferred_element_type=jnp.float32)
    q_all = lax.all_gather(query.reshape(rows, width_loc), "kv", axis=1, tiled=True)
    local_cache = cache[0]
    slots_here = local_cache.shape[0]
    slot_ids = me_kv * slots_here + jnp.arange(slots_here, dtype=jnp.int32)
    match = (page_table[None, :, :] == slot_ids[:, None, None]).astype(jnp.int32)
    owner_req = jnp.sum(
        match * jnp.arange(groups_here, dtype=jnp.int32)[None, :, None], axis=(1, 2)
    )
    owner_page = jnp.sum(
        match * jnp.arange(page_table.shape[1], dtype=jnp.int32)[None, None, :], axis=(1, 2)
    )
    page_pos = jnp.arange(PAGE, dtype=jnp.int32)
    reqs = jnp.arange(groups_here, dtype=jnp.int32)
    live = (owner_req[None, :, None] == reqs[:, None, None]) & (
        owner_page[None, :, None] * PAGE + page_pos[None, None, :] < cached_len[:, None, None]
    )
    live = live.astype(jnp.int32).reshape(groups_here, 1, slots_here * PAGE)
    accums, tops, totals = attend_pages(q_all, local_cache, live)
    tops = tops.reshape(HEADS, groups_here, span_rows)
    totals = totals.reshape(HEADS, groups_here, span_rows)
    top_new = jnp.transpose(top_new, (1, 0, 2))
    total_new = jnp.transpose(total_new, (1, 0, 2))
    accum_new = jnp.transpose(accum_new, (1, 0, 2, 3))
    own = lax.dynamic_slice_in_dim(tops, me_kv * heads_loc, heads_loc, 0)
    with_new = lax.dynamic_update_slice_in_dim(
        tops, jnp.maximum(own, top_new), me_kv * heads_loc, 0
    )
    largest = jnp.max(lax.all_gather(with_new, "kv", axis=0, tiled=False), axis=0)
    factor = jnp.exp(tops - largest)
    tot_rows = (totals * factor).reshape(HEADS, groups_here, span_rows // HD, HD)
    packed = jnp.concatenate([accums * factor[..., None], tot_rows], axis=2)
    summed = lax.psum_scatter(packed, "kv", scatter_dimension=0, tiled=True)
    sum_acc = summed[:, :, :span_rows]
    sum_tot = summed[:, :, span_rows:].reshape(heads_loc, groups_here, span_rows)
    own_largest = lax.dynamic_slice_in_dim(largest, me_kv * heads_loc, heads_loc, 0)
    fresh = jnp.exp(top_new - own_largest)
    numer = sum_acc + accum_new * fresh[..., None]
    denom = sum_tot + total_new * fresh
    att = (numer / denom[..., None]).astype(jnp.bfloat16)
    att = jnp.transpose(att, (1, 2, 0, 3)).reshape(rows, width_loc)
    hidden = jax.nn.gelu(up_acc, approximate=False).astype(jnp.bfloat16)
    dense_piece = lax.all_gather(dense_weight, "req", axis=1, tiled=True)
    down_piece = lax.all_gather(down_weight, "req", axis=1, tiled=True)
    value = jnp.dot(att, dense_piece, preferred_element_type=jnp.float32) + jnp.dot(
        hidden, down_piece, preferred_element_type=jnp.float32
    )
    summed = lax.psum_scatter(value, "kv", scatter_dimension=1, tiled=True)
    width_out = D // n_kv
    residual = lax.dynamic_slice_in_dim(x, me_kv * width_out, width_out, 1)
    return residual + summed


def solution(mesh):
    placed = (
        P("req", None),
        P(),
        P("req", None, "kv"),
        P("kv", "req"),
        P("req", "kv"),
        P("kv", "req"),
        P("req", "kv", None, None, None, None),
        P("req"),
        P("req", None),
    )
    return jax.shard_map(
        per_device, mesh=mesh, in_specs=placed, out_specs=P("req", "kv"), check_vma=False
    )
```

```python
import jax
import jax.numpy as jnp
from jax import lax
from jax.sharding import PartitionSpec as P
from jax.experimental import pallas as pl

D = 4096
HEADS = 32
HD = 128
ROT = 32
PAGE = 128
KV = ("z", "xh", "y")


def head_slot(h, nz, nxh, ny):
    return (h % ny * nz + h // (nxh * ny)) * nxh + h // ny % nxh


def by_slot(w, split):
    nz, nxh, ny = split
    lead = w.shape[0]
    blocks = w.reshape(lead, nz, nxh, ny, w.shape[1] // (nz * nxh * ny))
    return jnp.transpose(blocks, (0, 3, 1, 2, 4)).reshape(w.shape)


def scatter_staged(x, dim):
    for name in ("y", "z", "xh"):
        x = lax.psum_scatter(x, name, scatter_dimension=dim, tiled=True)
    return x


def gather_staged(x, dim):
    for name in ("y", "xh", "z"):
        x = lax.all_gather(x, name, axis=dim, tiled=True)
    return x


def max_staged(x):
    for name in ("y", "xh", "z"):
        x = jnp.max(lax.all_gather(x, name, axis=0, tiled=False), axis=0)
    return x


def layer_norm(x, gain):
    mean = jnp.mean(x, axis=-1, keepdims=True)
    cent = x - mean
    var = jnp.mean(cent * cent, axis=-1, keepdims=True)
    return cent * lax.rsqrt(var + 1e-05) * gain


def rotate(t, pos):
    half = ROT // 2
    freq = 10000.0 ** (-(jnp.arange(half, dtype=jnp.float32) * 2.0 / ROT))
    angle = pos[:, None] * freq[None, :]
    cosine = jnp.cos(angle)[:, None, :]
    sine = jnp.sin(angle)[:, None, :]
    first = t[..., :half]
    second = t[..., half:ROT]
    return jnp.concatenate(
        [first * cosine - second * sine, second * cosine + first * sine, t[..., ROT:]], axis=-1
    )


def attend_kernel(q_ref, k_ref, v_ref, live_ref, acc_ref, top_ref, tot_ref):
    scale = 1.0 / HD**0.5
    slots = k_ref.shape[0]
    q = q_ref[...]
    k = k_ref[...].reshape(slots * PAGE, HD)
    v = v_ref[...].reshape(slots * PAGE, HD)
    scores = (
        lax.dot_general(q, k, (((1,), (1,)), ((), ())), preferred_element_type=jnp.float32)
        * scale
    )
    live = live_ref[...] > 0
    top = jnp.max(jnp.where(live, scores, -1e30), axis=1, keepdims=True)
    weights = jnp.where(live, jnp.exp(scores - top), 0.0).astype(jnp.bfloat16)
    tot_ref[...] = jnp.sum(weights.astype(jnp.float32), axis=1, keepdims=True)
    top_ref[...] = top
    acc_ref[...] = jnp.dot(weights, v, preferred_element_type=jnp.float32)


def attend_pages(q_all, local_cache, live, split):
    groups, span = live.shape[0], q_all.shape[0] // live.shape[0]
    slots = local_cache.shape[0]
    heads = local_cache.shape[2]
    page_spec = lambda kv: pl.BlockSpec(
        (slots, None, None, PAGE, HD), lambda g, h: (0, kv, h, 0, 0)
    )
    return pl.pallas_call(
        attend_kernel,
        grid=(groups, heads),
        in_specs=[
            pl.BlockSpec((span, HD), lambda g, h: (g, h)),
            page_spec(0),
            page_spec(1),
            pl.BlockSpec((None, 1, slots * PAGE), lambda g, h: (g, 0, 0)),
        ],
        out_specs=[
            pl.BlockSpec((None, None, span, HD), lambda g, h: (head_slot(h, *split), g, 0, 0)),
            pl.BlockSpec((None, None, span, 1), lambda g, h: (head_slot(h, *split), g, 0, 0)),
            pl.BlockSpec((None, None, span, 1), lambda g, h: (head_slot(h, *split), g, 0, 0)),
        ],
        out_shape=[
            jax.ShapeDtypeStruct((heads, groups, span, HD), jnp.float32),
            jax.ShapeDtypeStruct((heads, groups, span, 1), jnp.float32),
            jax.ShapeDtypeStruct((heads, groups, span, 1), jnp.float32),
        ],
        cost_estimate=pl.CostEstimate(
            flops=4 * groups * heads * span * slots * PAGE * HD,
            transcendentals=groups * heads * span * slots * PAGE,
            bytes_accessed=groups * local_cache.size * 2 + q_all.size * 2
            + groups * heads * span * HD * 4,
        ),
    )(q_all, local_cache, local_cache, live)


def per_device(
    hidden_in,
    ln_gains,
    qkv_weight,
    dense_weight,
    up_weight,
    down_weight,
    cache,
    cached_len,
    page_table,
):
    split = tuple(lax.axis_size(name) for name in KV)
    n_kv = split[0] * split[1] * split[2]
    me_kv = lax.axis_index(KV)
    slot_me = head_slot(me_kv, *split)
    rows = hidden_in.shape[0]
    groups_here = cached_len.shape[0]
    span_rows = rows // groups_here
    width_loc = qkv_weight.shape[2]
    heads_loc = width_loc // HD
    scale = 1.0 / HD**0.5
    x = hidden_in.astype(jnp.float32)
    h1 = layer_norm(x, ln_gains[0]).astype(jnp.bfloat16)
    h2 = layer_norm(x, ln_gains[1]).astype(jnp.bfloat16)
    qkv_piece = lax.all_gather(qkv_weight, "req", axis=0, tiled=True)
    up_piece = lax.all_gather(up_weight, "req", axis=0, tiled=True)
    count = qkv_piece.shape[0]
    qkv_acc = jnp.dot(
        h1, qkv_piece.reshape(count, 3 * width_loc), preferred_element_type=jnp.float32
    )
    up_acc = jnp.dot(h2, up_piece, preferred_element_type=jnp.float32)
    qkv = qkv_acc
    qkv = qkv.reshape(rows, 3, heads_loc, HD)
    offsets = jnp.arange(span_rows, dtype=jnp.int32)
    pos = (cached_len[:, None] + offsets[None, :]).reshape(rows).astype(jnp.float32)
    query = rotate(qkv[:, 0], pos).astype(jnp.bfloat16)
    key_new = rotate(qkv[:, 1], pos).astype(jnp.bfloat16)
    value_new = qkv[:, 2].astype(jnp.bfloat16)
    q_grp = query.reshape(groups_here, span_rows, heads_loc, HD)
    k_grp = key_new.reshape(groups_here, span_rows, heads_loc, HD)
    v_grp = value_new.reshape(groups_here, span_rows, heads_loc, HD)
    causal = offsets[None, :] <= offsets[:, None]
    s_new = jnp.einsum("gqhd,gkhd->ghqk", q_grp, k_grp, preferred_element_type=jnp.float32) * scale
    s_new = jnp.where(causal[None, None], s_new, -1e30)
    top_new = jnp.max(s_new, axis=-1)
    p_new = jnp.where(causal[None, None], jnp.exp(s_new - top_new[..., None]), 0.0).astype(
        jnp.bfloat16
    )
    total_new = jnp.sum(p_new.astype(jnp.float32), axis=-1)
    accum_new = jnp.einsum("ghqk,gkhd->ghqd", p_new, v_grp, preferred_element_type=jnp.float32)
    q_all = gather_staged(query.reshape(rows, width_loc), 1)
    local_cache = cache[0]
    slots_here = local_cache.shape[0]
    slot_ids = me_kv * slots_here + jnp.arange(slots_here, dtype=jnp.int32)
    match = (page_table[None, :, :] == slot_ids[:, None, None]).astype(jnp.int32)
    owner_req = jnp.sum(
        match * jnp.arange(groups_here, dtype=jnp.int32)[None, :, None], axis=(1, 2)
    )
    owner_page = jnp.sum(
        match * jnp.arange(page_table.shape[1], dtype=jnp.int32)[None, None, :], axis=(1, 2)
    )
    page_pos = jnp.arange(PAGE, dtype=jnp.int32)
    reqs = jnp.arange(groups_here, dtype=jnp.int32)
    live = (owner_req[None, :, None] == reqs[:, None, None]) & (
        owner_page[None, :, None] * PAGE + page_pos[None, None, :] < cached_len[:, None, None]
    )
    live = live.astype(jnp.int32).reshape(groups_here, 1, slots_here * PAGE)
    accums, tops, totals = attend_pages(q_all, local_cache, live, split)
    tops = tops.reshape(HEADS, groups_here, span_rows)
    totals = totals.reshape(HEADS, groups_here, span_rows)
    top_new = jnp.transpose(top_new, (1, 0, 2))
    total_new = jnp.transpose(total_new, (1, 0, 2))
    accum_new = jnp.transpose(accum_new, (1, 0, 2, 3))
    own = lax.dynamic_slice_in_dim(tops, slot_me, heads_loc, 0)
    with_new = lax.dynamic_update_slice_in_dim(tops, jnp.maximum(own, top_new), slot_me, 0)
    largest = max_staged(with_new)
    factor = jnp.exp(tops - largest)
    tot_rows = (totals * factor).reshape(HEADS, groups_here, span_rows // HD, HD)
    packed = jnp.concatenate([accums * factor[..., None], tot_rows], axis=2)
    summed = scatter_staged(packed, 0)
    sum_acc = summed[:, :, :span_rows]
    sum_tot = summed[:, :, span_rows:].reshape(heads_loc, groups_here, span_rows)
    own_largest = lax.dynamic_slice_in_dim(largest, slot_me, heads_loc, 0)
    fresh = jnp.exp(top_new - own_largest)
    numer = sum_acc + accum_new * fresh[..., None]
    denom = sum_tot + total_new * fresh
    att = (numer / denom[..., None]).astype(jnp.bfloat16)
    att = jnp.transpose(att, (1, 2, 0, 3)).reshape(rows, width_loc)
    hidden = jax.nn.gelu(up_acc, approximate=False).astype(jnp.bfloat16)
    dense_piece = by_slot(lax.all_gather(dense_weight, "req", axis=1, tiled=True), split)
    down_piece = by_slot(lax.all_gather(down_weight, "req", axis=1, tiled=True), split)
    value = jnp.dot(att, dense_piece, preferred_element_type=jnp.float32) + jnp.dot(
        hidden, down_piece, preferred_element_type=jnp.float32
    )
    summed = scatter_staged(value, 1)
    width_out = D // n_kv
    residual = lax.dynamic_slice_in_dim(x, me_kv * width_out, width_out, 1)
    return residual + summed


def solution(mesh):
    kv_split = (4, 2, 4)
    devices = mesh.devices.reshape((mesh.shape["req"],) + kv_split)
    torus = jax.sharding.Mesh(devices, ("req",) + KV)
    placed = (
        P("req", None),
        P(),
        P("req", None, KV),
        P(KV, "req"),
        P("req", KV),
        P(KV, "req"),
        P("req", KV, None, None, None, None),
        P("req"),
        P("req", None),
    )
    return jax.shard_map(
        per_device, mesh=torus, in_specs=placed, out_specs=P("req", KV), check_vma=False
    )
```

```python
import jax
import jax.numpy as jnp
from jax import lax
from jax.sharding import PartitionSpec as P
from jax.experimental import pallas as pl

D = 4096
HEADS = 32
HD = 128
ROT = 32
PAGE = 128
KV = ("z", "xh", "y")


def head_slot(h, nz, nxh, ny):
    return (h % ny * nz + h // (nxh * ny)) * nxh + h // ny % nxh


def by_slot(w, split):
    nz, nxh, ny = split
    lead = w.shape[0]
    blocks = w.reshape(lead, nz, nxh, ny, w.shape[1] // (nz * nxh * ny))
    return jnp.transpose(blocks, (0, 3, 1, 2, 4)).reshape(w.shape)


def scatter_staged(x, dim):
    for name in ("y", "z", "xh"):
        x = lax.psum_scatter(x, name, scatter_dimension=dim, tiled=True)
    return x


def gather_staged(x, dim):
    for name in ("y", "xh", "z"):
        x = lax.all_gather(x, name, axis=dim, tiled=True)
    return x


def max_staged(x):
    for name in ("y", "xh", "z"):
        x = jnp.max(lax.all_gather(x, name, axis=0, tiled=False), axis=0)
    return x


def layer_norm(x, gain):
    mean = jnp.mean(x, axis=-1, keepdims=True)
    cent = x - mean
    var = jnp.mean(cent * cent, axis=-1, keepdims=True)
    return cent * lax.rsqrt(var + 1e-05) * gain


def rotate(t, pos):
    half = ROT // 2
    freq = 10000.0 ** (-(jnp.arange(half, dtype=jnp.float32) * 2.0 / ROT))
    angle = pos[:, None] * freq[None, :]
    cosine = jnp.cos(angle)[:, None, :]
    sine = jnp.sin(angle)[:, None, :]
    first = t[..., :half]
    second = t[..., half:ROT]
    return jnp.concatenate(
        [first * cosine - second * sine, second * cosine + first * sine, t[..., ROT:]], axis=-1
    )


def attend_kernel(q_ref, k_ref, v_ref, live_ref, acc_ref, top_ref, tot_ref):
    scale = 1.0 / HD**0.5
    slots = k_ref.shape[0]
    q = q_ref[...]
    k = k_ref[...].reshape(slots * PAGE, HD)
    v = v_ref[...].reshape(slots * PAGE, HD)
    scores = (
        lax.dot_general(q, k, (((1,), (1,)), ((), ())), preferred_element_type=jnp.float32)
        * scale
    )
    live = live_ref[...] > 0
    top = jnp.max(jnp.where(live, scores, -1e30), axis=1, keepdims=True)
    weights = jnp.where(live, jnp.exp(scores - top), 0.0).astype(jnp.bfloat16)
    tot_ref[...] = jnp.sum(weights.astype(jnp.float32), axis=1, keepdims=True)
    top_ref[...] = top
    acc_ref[...] = jnp.dot(weights, v, preferred_element_type=jnp.float32)


def attend_pages(q_all, local_cache, live, split):
    groups, span = live.shape[0], q_all.shape[0] // live.shape[0]
    slots = local_cache.shape[0]
    heads = local_cache.shape[2]
    page_spec = lambda kv: pl.BlockSpec(
        (slots, None, None, PAGE, HD), lambda g, h: (0, kv, h, 0, 0)
    )
    return pl.pallas_call(
        attend_kernel,
        grid=(groups, heads),
        in_specs=[
            pl.BlockSpec((span, HD), lambda g, h: (g, h)),
            page_spec(0),
            page_spec(1),
            pl.BlockSpec((None, 1, slots * PAGE), lambda g, h: (g, 0, 0)),
        ],
        out_specs=[
            pl.BlockSpec((None, None, span, HD), lambda g, h: (head_slot(h, *split), g, 0, 0)),
            pl.BlockSpec((None, None, span, 1), lambda g, h: (head_slot(h, *split), g, 0, 0)),
            pl.BlockSpec((None, None, span, 1), lambda g, h: (head_slot(h, *split), g, 0, 0)),
        ],
        out_shape=[
            jax.ShapeDtypeStruct((heads, groups, span, HD), jnp.float32),
            jax.ShapeDtypeStruct((heads, groups, span, 1), jnp.float32),
            jax.ShapeDtypeStruct((heads, groups, span, 1), jnp.float32),
        ],
        cost_estimate=pl.CostEstimate(
            flops=4 * groups * heads * span * slots * PAGE * HD,
            transcendentals=groups * heads * span * slots * PAGE,
            bytes_accessed=groups * local_cache.size * 2 + q_all.size * 2
            + groups * heads * span * HD * 4,
        ),
    )(q_all, local_cache, local_cache, live)


def per_device(
    hidden_in,
    ln_gains,
    qkv_weight,
    dense_weight,
    up_weight,
    down_weight,
    cache,
    cached_len,
    page_table,
):
    split = tuple(lax.axis_size(name) for name in KV)
    n_kv = split[0] * split[1] * split[2]
    me_kv = lax.axis_index(KV)
    slot_me = head_slot(me_kv, *split)
    rows = hidden_in.shape[0]
    groups_here = cached_len.shape[0]
    span_rows = rows // groups_here
    width_loc = qkv_weight.shape[2]
    heads_loc = width_loc // HD
    scale = 1.0 / HD**0.5
    x = hidden_in.astype(jnp.float32)
    h1 = layer_norm(x, ln_gains[0]).astype(jnp.bfloat16)
    h2 = layer_norm(x, ln_gains[1]).astype(jnp.bfloat16)
    qkv_piece = lax.all_gather(qkv_weight, "req", axis=0, tiled=True)
    count = qkv_piece.shape[0]
    qkv_acc = jnp.dot(
        h1, qkv_piece.reshape(count, 3 * width_loc), preferred_element_type=jnp.float32
    )
    qkv = qkv_acc
    qkv = qkv.reshape(rows, 3, heads_loc, HD)
    offsets = jnp.arange(span_rows, dtype=jnp.int32)
    pos = (cached_len[:, None] + offsets[None, :]).reshape(rows).astype(jnp.float32)
    query = rotate(qkv[:, 0], pos).astype(jnp.bfloat16)
    key_new = rotate(qkv[:, 1], pos).astype(jnp.bfloat16)
    value_new = qkv[:, 2].astype(jnp.bfloat16)
    q_grp = query.reshape(groups_here, span_rows, heads_loc, HD)
    k_grp = key_new.reshape(groups_here, span_rows, heads_loc, HD)
    v_grp = value_new.reshape(groups_here, span_rows, heads_loc, HD)
    causal = offsets[None, :] <= offsets[:, None]
    s_new = jnp.einsum("gqhd,gkhd->ghqk", q_grp, k_grp, preferred_element_type=jnp.float32) * scale
    s_new = jnp.where(causal[None, None], s_new, -1e30)
    top_new = jnp.max(s_new, axis=-1)
    p_new = jnp.where(causal[None, None], jnp.exp(s_new - top_new[..., None]), 0.0).astype(
        jnp.bfloat16
    )
    total_new = jnp.sum(p_new.astype(jnp.float32), axis=-1)
    accum_new = jnp.einsum("ghqk,gkhd->ghqd", p_new, v_grp, preferred_element_type=jnp.float32)
    q_all = gather_staged(query.reshape(rows, width_loc), 1)
    up_weight, dense_weight, down_weight, q_all = lax.optimization_barrier(
        (up_weight, dense_weight, down_weight, q_all)
    )
    up_piece = lax.all_gather(up_weight, "req", axis=0, tiled=True)
    dense_piece = by_slot(lax.all_gather(dense_weight, "req", axis=1, tiled=True), split)
    down_piece = by_slot(lax.all_gather(down_weight, "req", axis=1, tiled=True), split)
    local_cache = cache[0]
    slots_here = local_cache.shape[0]
    slot_ids = me_kv * slots_here + jnp.arange(slots_here, dtype=jnp.int32)
    match = (page_table[None, :, :] == slot_ids[:, None, None]).astype(jnp.int32)
    owner_req = jnp.sum(
        match * jnp.arange(groups_here, dtype=jnp.int32)[None, :, None], axis=(1, 2)
    )
    owner_page = jnp.sum(
        match * jnp.arange(page_table.shape[1], dtype=jnp.int32)[None, None, :], axis=(1, 2)
    )
    page_pos = jnp.arange(PAGE, dtype=jnp.int32)
    reqs = jnp.arange(groups_here, dtype=jnp.int32)
    live = (owner_req[None, :, None] == reqs[:, None, None]) & (
        owner_page[None, :, None] * PAGE + page_pos[None, None, :] < cached_len[:, None, None]
    )
    live = live.astype(jnp.int32).reshape(groups_here, 1, slots_here * PAGE)
    accums, tops, totals = attend_pages(q_all, local_cache, live, split)
    tops = tops.reshape(HEADS, groups_here, span_rows)
    totals = totals.reshape(HEADS, groups_here, span_rows)
    top_new = jnp.transpose(top_new, (1, 0, 2))
    total_new = jnp.transpose(total_new, (1, 0, 2))
    accum_new = jnp.transpose(accum_new, (1, 0, 2, 3))
    own = lax.dynamic_slice_in_dim(tops, slot_me, heads_loc, 0)
    with_new = lax.dynamic_update_slice_in_dim(tops, jnp.maximum(own, top_new), slot_me, 0)
    largest = max_staged(with_new)
    factor = jnp.exp(tops - largest)
    tot_rows = (totals * factor).reshape(HEADS, groups_here, span_rows // HD, HD)
    packed = jnp.concatenate([accums * factor[..., None], tot_rows], axis=2)
    packed, up_piece, dense_piece, down_piece = lax.optimization_barrier(
        (packed, up_piece, dense_piece, down_piece)
    )
    summed = scatter_staged(packed, 0)
    sum_acc = summed[:, :, :span_rows]
    sum_tot = summed[:, :, span_rows:].reshape(heads_loc, groups_here, span_rows)
    own_largest = lax.dynamic_slice_in_dim(largest, slot_me, heads_loc, 0)
    fresh = jnp.exp(top_new - own_largest)
    numer = sum_acc + accum_new * fresh[..., None]
    denom = sum_tot + total_new * fresh
    att = (numer / denom[..., None]).astype(jnp.bfloat16)
    att = jnp.transpose(att, (1, 2, 0, 3)).reshape(rows, width_loc)
    up_acc = jnp.dot(h2, up_piece, preferred_element_type=jnp.float32)
    hidden = jax.nn.gelu(up_acc, approximate=False).astype(jnp.bfloat16)
    value = jnp.dot(att, dense_piece, preferred_element_type=jnp.float32) + jnp.dot(
        hidden, down_piece, preferred_element_type=jnp.float32
    )
    summed = scatter_staged(value, 1)
    width_out = D // n_kv
    residual = lax.dynamic_slice_in_dim(x, me_kv * width_out, width_out, 1)
    return residual + summed


def solution(mesh):
    kv_split = (4, 2, 4)
    devices = mesh.devices.reshape((mesh.shape["req"],) + kv_split)
    torus = jax.sharding.Mesh(devices, ("req",) + KV)
    placed = (
        P("req", None),
        P(),
        P("req", None, KV),
        P(KV, "req"),
        P("req", KV),
        P(KV, "req"),
        P("req", KV, None, None, None, None),
        P("req"),
        P("req", None),
    )
    return jax.shard_map(
        per_device, mesh=torus, in_specs=placed, out_specs=P("req", KV), check_vma=False
    )
```

```python
import jax
import jax.numpy as jnp
from jax import lax
from jax.sharding import PartitionSpec as P
from jax.experimental import pallas as pl

D = 4096
HEADS = 32
HD = 128
ROT = 32
PAGE = 128
KV = ("z", "xh", "y")


def head_slot(h, nz, nxh, ny):
    return (h % ny * nz + h // (nxh * ny)) * nxh + h // ny % nxh


def by_slot(w, split):
    nz, nxh, ny = split
    lead = w.shape[0]
    blocks = w.reshape(lead, nz, nxh, ny, w.shape[1] // (nz * nxh * ny))
    return jnp.transpose(blocks, (0, 3, 1, 2, 4)).reshape(w.shape)


def scatter_staged(x, dim):
    for name in ("y", "z", "xh"):
        x = lax.psum_scatter(x, name, scatter_dimension=dim, tiled=True)
    return x


def gather_staged(x, dim):
    for name in ("y", "xh", "z"):
        x = lax.all_gather(x, name, axis=dim, tiled=True)
    return x


def max_staged(x):
    for name in ("y", "xh", "z"):
        x = jnp.max(lax.all_gather(x, name, axis=0, tiled=False), axis=0)
    return x


def layer_norm(x, gain):
    mean = jnp.mean(x, axis=-1, keepdims=True)
    cent = x - mean
    var = jnp.mean(cent * cent, axis=-1, keepdims=True)
    return cent * lax.rsqrt(var + 1e-05) * gain


def rotate(t, pos):
    half = ROT // 2
    freq = 10000.0 ** (-(jnp.arange(half, dtype=jnp.float32) * 2.0 / ROT))
    angle = pos[:, None] * freq[None, :]
    cosine = jnp.cos(angle)[:, None, :]
    sine = jnp.sin(angle)[:, None, :]
    first = t[..., :half]
    second = t[..., half:ROT]
    return jnp.concatenate(
        [first * cosine - second * sine, second * cosine + first * sine, t[..., ROT:]], axis=-1
    )


def attend_kernel(q_ref, k_ref, v_ref, live_ref, acc_ref, top_ref, tot_ref):
    scale = 1.0 / HD**0.5
    slots = k_ref.shape[0]
    q = q_ref[...]
    k = k_ref[...].reshape(slots * PAGE, HD)
    v = v_ref[...].reshape(slots * PAGE, HD)
    scores = (
        lax.dot_general(k, q, (((1,), (1,)), ((), ())), preferred_element_type=jnp.float32)
        * scale
    )
    live = live_ref[...] > 0
    top = jnp.max(jnp.where(live, scores, -1e30), axis=0, keepdims=True)
    weights = jnp.where(live, jnp.exp(scores - top), 0.0).astype(jnp.bfloat16)
    tot_ref[...] = jnp.sum(weights.astype(jnp.float32), axis=0, keepdims=True)
    top_ref[...] = top
    acc_ref[...] = lax.dot_general(
        weights, v, (((0,), (0,)), ((), ())), preferred_element_type=jnp.float32
    )


def attend_pages(q_all, local_cache, live, split):
    groups, span = live.shape[0], q_all.shape[0] // live.shape[0]
    slots = local_cache.shape[0]
    heads = local_cache.shape[2]
    page_spec = lambda kv: pl.BlockSpec(
        (slots, None, None, PAGE, HD), lambda g, h: (0, kv, h, 0, 0)
    )
    row_spec = pl.BlockSpec((None, None, 1, span), lambda g, h: (head_slot(h, *split), g, 0, 0))
    return pl.pallas_call(
        attend_kernel,
        grid=(groups, heads),
        in_specs=[
            pl.BlockSpec((span, HD), lambda g, h: (g, h)),
            page_spec(0),
            page_spec(1),
            pl.BlockSpec((None, slots * PAGE, 1), lambda g, h: (g, 0, 0)),
        ],
        out_specs=[
            pl.BlockSpec((None, None, span, HD), lambda g, h: (head_slot(h, *split), g, 0, 0)),
            row_spec,
            row_spec,
        ],
        out_shape=[
            jax.ShapeDtypeStruct((heads, groups, span, HD), jnp.float32),
            jax.ShapeDtypeStruct((heads, groups, 1, span), jnp.float32),
            jax.ShapeDtypeStruct((heads, groups, 1, span), jnp.float32),
        ],
        cost_estimate=pl.CostEstimate(
            flops=4 * groups * heads * span * slots * PAGE * HD,
            transcendentals=groups * heads * span * slots * PAGE,
            bytes_accessed=groups * local_cache.size * 2 + q_all.size * 2
            + groups * heads * span * HD * 4,
        ),
    )(q_all, local_cache, local_cache, live)


def per_device(
    hidden_in,
    ln_gains,
    qkv_weight,
    dense_weight,
    up_weight,
    down_weight,
    cache,
    cached_len,
    page_table,
):
    split = tuple(lax.axis_size(name) for name in KV)
    n_kv = split[0] * split[1] * split[2]
    me_kv = lax.axis_index(KV)
    slot_me = head_slot(me_kv, *split)
    rows = hidden_in.shape[0]
    groups_here = cached_len.shape[0]
    span_rows = rows // groups_here
    width_loc = qkv_weight.shape[2]
    heads_loc = width_loc // HD
    scale = 1.0 / HD**0.5
    x = hidden_in.astype(jnp.float32)
    h1 = layer_norm(x, ln_gains[0]).astype(jnp.bfloat16)
    h2 = layer_norm(x, ln_gains[1]).astype(jnp.bfloat16)
    q_piece = lax.all_gather(qkv_weight[:, 0], "req", axis=0, tiled=True)
    q_acc = jnp.dot(h1, q_piece, preferred_element_type=jnp.float32)
    offsets = jnp.arange(span_rows, dtype=jnp.int32)
    pos = (cached_len[:, None] + offsets[None, :]).reshape(rows).astype(jnp.float32)
    query = rotate(q_acc.reshape(rows, heads_loc, HD), pos).astype(jnp.bfloat16)
    q_all = gather_staged(query.reshape(rows, width_loc), 1)
    kv_weight, q_all = lax.optimization_barrier((qkv_weight[:, 1:], q_all))
    kv_piece = lax.all_gather(kv_weight, "req", axis=0, tiled=True)
    count = kv_piece.shape[0]
    kv_acc = jnp.dot(
        h1, kv_piece.reshape(count, 2 * width_loc), preferred_element_type=jnp.float32
    ).reshape(rows, 2, heads_loc, HD)
    key_new = rotate(kv_acc[:, 0], pos).astype(jnp.bfloat16)
    value_new = kv_acc[:, 1].astype(jnp.bfloat16)
    q_grp = query.reshape(groups_here, span_rows, heads_loc, HD)
    k_grp = key_new.reshape(groups_here, span_rows, heads_loc, HD)
    v_grp = value_new.reshape(groups_here, span_rows, heads_loc, HD)
    causal = offsets[None, :] <= offsets[:, None]
    s_new = jnp.einsum("gqhd,gkhd->ghqk", q_grp, k_grp, preferred_element_type=jnp.float32) * scale
    s_new = jnp.where(causal[None, None], s_new, -1e30)
    top_new = jnp.max(s_new, axis=-1)
    p_new = jnp.where(causal[None, None], jnp.exp(s_new - top_new[..., None]), 0.0).astype(
        jnp.bfloat16
    )
    total_new = jnp.sum(p_new.astype(jnp.float32), axis=-1)
    accum_new = jnp.einsum("ghqk,gkhd->ghqd", p_new, v_grp, preferred_element_type=jnp.float32)
    up_weight, dense_weight, down_weight, kv_piece = lax.optimization_barrier(
        (up_weight, dense_weight, down_weight, kv_piece)
    )
    up_piece = lax.all_gather(up_weight, "req", axis=0, tiled=True)
    dense_piece = by_slot(lax.all_gather(dense_weight, "req", axis=1, tiled=True), split)
    down_piece = by_slot(lax.all_gather(down_weight, "req", axis=1, tiled=True), split)
    local_cache = cache[0]
    slots_here = local_cache.shape[0]
    slot_ids = me_kv * slots_here + jnp.arange(slots_here, dtype=jnp.int32)
    match = (page_table[None, :, :] == slot_ids[:, None, None]).astype(jnp.int32)
    owner_req = jnp.sum(
        match * jnp.arange(groups_here, dtype=jnp.int32)[None, :, None], axis=(1, 2)
    )
    owner_page = jnp.sum(
        match * jnp.arange(page_table.shape[1], dtype=jnp.int32)[None, None, :], axis=(1, 2)
    )
    page_pos = jnp.arange(PAGE, dtype=jnp.int32)
    reqs = jnp.arange(groups_here, dtype=jnp.int32)
    live = (owner_req[None, :, None] == reqs[:, None, None]) & (
        owner_page[None, :, None] * PAGE + page_pos[None, None, :] < cached_len[:, None, None]
    )
    live = live.astype(jnp.int32).reshape(groups_here, slots_here * PAGE, 1)
    accums, tops, totals = attend_pages(q_all, local_cache, live, split)
    tops = tops.reshape(HEADS, groups_here, span_rows)
    totals = totals.reshape(HEADS, groups_here, span_rows)
    top_new = jnp.transpose(top_new, (1, 0, 2))
    total_new = jnp.transpose(total_new, (1, 0, 2))
    accum_new = jnp.transpose(accum_new, (1, 0, 2, 3))
    own = lax.dynamic_slice_in_dim(tops, slot_me, heads_loc, 0)
    with_new = lax.dynamic_update_slice_in_dim(tops, jnp.maximum(own, top_new), slot_me, 0)
    largest = max_staged(with_new)
    factor = jnp.exp(tops - largest)
    tot_rows = (totals * factor).reshape(HEADS, groups_here, span_rows // HD, HD)
    packed = jnp.concatenate([accums * factor[..., None], tot_rows], axis=2)
    packed, up_piece, dense_piece, down_piece = lax.optimization_barrier(
        (packed, up_piece, dense_piece, down_piece)
    )
    summed = lax.psum_scatter(packed, "y", scatter_dimension=0, tiled=True)
    up_acc = jnp.dot(h2, up_piece, preferred_element_type=jnp.float32)
    hidden = jax.nn.gelu(up_acc, approximate=False).astype(jnp.bfloat16)
    mlp = jnp.dot(hidden, down_piece, preferred_element_type=jnp.float32)
    summed, mlp = lax.optimization_barrier((summed, mlp))
    for name in ("z", "xh"):
        summed = lax.psum_scatter(summed, name, scatter_dimension=0, tiled=True)
    sum_acc = summed[:, :, :span_rows]
    sum_tot = summed[:, :, span_rows:].reshape(heads_loc, groups_here, span_rows)
    own_largest = lax.dynamic_slice_in_dim(largest, slot_me, heads_loc, 0)
    fresh = jnp.exp(top_new - own_largest)
    numer = sum_acc + accum_new * fresh[..., None]
    denom = sum_tot + total_new * fresh
    att = (numer / denom[..., None]).astype(jnp.bfloat16)
    att = jnp.transpose(att, (1, 2, 0, 3)).reshape(rows, width_loc)
    value = jnp.dot(att, dense_piece, preferred_element_type=jnp.float32) + mlp
    summed = scatter_staged(value, 1)
    width_out = D // n_kv
    residual = lax.dynamic_slice_in_dim(x, me_kv * width_out, width_out, 1)
    return residual + summed


def solution(mesh):
    kv_split = (4, 2, 4)
    devices = mesh.devices.reshape((mesh.shape["req"],) + kv_split)
    torus = jax.sharding.Mesh(devices, ("req",) + KV)
    placed = (
        P("req", None),
        P(),
        P("req", None, KV),
        P(KV, "req"),
        P("req", KV),
        P(KV, "req"),
        P("req", KV, None, None, None, None),
        P("req"),
        P("req", None),
    )
    return jax.shard_map(
        per_device, mesh=torus, in_specs=placed, out_specs=P("req", KV), check_vma=False
    )
```

```python
import jax
import jax.numpy as jnp
from jax import lax
from jax.sharding import PartitionSpec as P
from jax.experimental import pallas as pl

D = 4096
HEADS = 32
HD = 128
ROT = 32
PAGE = 128
KV = ("z", "xh", "y")


def head_slot(h, nz, nxh, ny):
    return (h % ny * nz + h // (nxh * ny)) * nxh + h // ny % nxh


def by_slot(w, split):
    nz, nxh, ny = split
    lead = w.shape[0]
    blocks = w.reshape(lead, nz, nxh, ny, w.shape[1] // (nz * nxh * ny))
    return jnp.transpose(blocks, (0, 3, 1, 2, 4)).reshape(w.shape)


def scatter_staged(x, dim):
    for name in ("y", "z", "xh"):
        x = lax.psum_scatter(x, name, scatter_dimension=dim, tiled=True)
    return x


def gather_staged(x, dim):
    for name in ("y", "xh", "z"):
        x = lax.all_gather(x, name, axis=dim, tiled=True)
    return x


def max_staged(x):
    for name in ("y", "xh", "z"):
        x = jnp.max(lax.all_gather(x, name, axis=0, tiled=False), axis=0)
    return x


def layer_norm(x, gain):
    mean = jnp.mean(x, axis=-1, keepdims=True)
    cent = x - mean
    var = jnp.mean(cent * cent, axis=-1, keepdims=True)
    return cent * lax.rsqrt(var + 1e-05) * gain


def rotate(t, pos):
    half = ROT // 2
    freq = 10000.0 ** (-(jnp.arange(half, dtype=jnp.float32) * 2.0 / ROT))
    angle = pos[:, None] * freq[None, :]
    cosine = jnp.cos(angle)[:, None, :]
    sine = jnp.sin(angle)[:, None, :]
    first = t[..., :half]
    second = t[..., half:ROT]
    return jnp.concatenate(
        [first * cosine - second * sine, second * cosine + first * sine, t[..., ROT:]], axis=-1
    )


def attend_kernel(q_ref, k_ref, v_ref, live_ref, acc_ref, top_ref, tot_ref):
    scale = 1.0 / HD**0.5
    slots = k_ref.shape[0]
    q = q_ref[...]
    k = k_ref[...].reshape(slots * PAGE, HD)
    v = v_ref[...].reshape(slots * PAGE, HD)
    scores = (
        lax.dot_general(k, q, (((1,), (1,)), ((), ())), preferred_element_type=jnp.float32)
        * scale
    )
    live = live_ref[...] > 0
    top = jnp.max(jnp.where(live, scores, -1e30), axis=0, keepdims=True)
    weights = jnp.where(live, jnp.exp(scores - top), 0.0).astype(jnp.bfloat16)
    tot_ref[...] = jnp.sum(weights.astype(jnp.float32), axis=0, keepdims=True)
    top_ref[...] = top
    acc_ref[...] = lax.dot_general(
        weights, v, (((0,), (0,)), ((), ())), preferred_element_type=jnp.float32
    )


def attend_pages(q_all, local_cache, live, split):
    groups, span = live.shape[0], q_all.shape[0] // live.shape[0]
    slots = local_cache.shape[0]
    heads = local_cache.shape[2]
    page_spec = lambda kv: pl.BlockSpec(
        (slots, None, None, PAGE, HD), lambda g, h: (0, kv, h, 0, 0)
    )
    row_spec = pl.BlockSpec((None, None, 1, span), lambda g, h: (head_slot(h, *split), g, 0, 0))
    return pl.pallas_call(
        attend_kernel,
        grid=(groups, heads),
        in_specs=[
            pl.BlockSpec((span, HD), lambda g, h: (g, h)),
            page_spec(0),
            page_spec(1),
            pl.BlockSpec((None, slots * PAGE, 1), lambda g, h: (g, 0, 0)),
        ],
        out_specs=[
            pl.BlockSpec((None, None, span, HD), lambda g, h: (head_slot(h, *split), g, 0, 0)),
            row_spec,
            row_spec,
        ],
        out_shape=[
            jax.ShapeDtypeStruct((heads, groups, span, HD), jnp.float32),
            jax.ShapeDtypeStruct((heads, groups, 1, span), jnp.float32),
            jax.ShapeDtypeStruct((heads, groups, 1, span), jnp.float32),
        ],
        cost_estimate=pl.CostEstimate(
            flops=4 * groups * heads * span * slots * PAGE * HD,
            transcendentals=groups * heads * span * slots * PAGE,
            bytes_accessed=groups * local_cache.size * 2 + q_all.size * 2
            + groups * heads * span * HD * 4,
        ),
    )(q_all, local_cache, local_cache, live)


def layer(
    hidden_in,
    ln_gains,
    qkv_weight,
    dense_weight,
    up_weight,
    down_weight,
    cache,
    cached_len,
    page_table,
):
    split = tuple(lax.axis_size(name) for name in KV)
    n_kv = split[0] * split[1] * split[2]
    me_kv = lax.axis_index(KV)
    slot_me = head_slot(me_kv, *split)
    rows = hidden_in.shape[0]
    groups_here = cached_len.shape[0]
    span_rows = rows // groups_here
    width_loc = qkv_weight.shape[2]
    heads_loc = width_loc // HD
    scale = 1.0 / HD**0.5
    x = hidden_in.astype(jnp.float32)
    h1 = layer_norm(x, ln_gains[0]).astype(jnp.bfloat16)
    h2 = layer_norm(x, ln_gains[1]).astype(jnp.bfloat16)
    q_piece = lax.all_gather(qkv_weight[:, 0], "req", axis=0, tiled=True)
    q_acc = jnp.dot(h1, q_piece, preferred_element_type=jnp.float32)
    offsets = jnp.arange(span_rows, dtype=jnp.int32)
    pos = (cached_len[:, None] + offsets[None, :]).reshape(rows).astype(jnp.float32)
    query = rotate(q_acc.reshape(rows, heads_loc, HD), pos).astype(jnp.bfloat16)
    q_all = gather_staged(query.reshape(rows, width_loc), 1)
    kv_weight, up_weight, dense_weight, down_weight, q_all = lax.optimization_barrier(
        (qkv_weight[:, 1:], up_weight, dense_weight, down_weight, q_all)
    )
    kv_piece = lax.all_gather(kv_weight, "req", axis=0, tiled=True)
    count = kv_piece.shape[0]
    kv_acc = jnp.dot(
        h1, kv_piece.reshape(count, 2 * width_loc), preferred_element_type=jnp.float32
    ).reshape(rows, 2, heads_loc, HD)
    key_new = rotate(kv_acc[:, 0], pos).astype(jnp.bfloat16)
    value_new = kv_acc[:, 1].astype(jnp.bfloat16)
    q_grp = query.reshape(groups_here, span_rows, heads_loc, HD)
    k_grp = key_new.reshape(groups_here, span_rows, heads_loc, HD)
    v_grp = value_new.reshape(groups_here, span_rows, heads_loc, HD)
    causal = offsets[None, :] <= offsets[:, None]
    s_new = jnp.einsum("gqhd,gkhd->ghqk", q_grp, k_grp, preferred_element_type=jnp.float32) * scale
    s_new = jnp.where(causal[None, None], s_new, -1e30)
    top_new = jnp.max(s_new, axis=-1)
    p_new = jnp.where(causal[None, None], jnp.exp(s_new - top_new[..., None]), 0.0).astype(
        jnp.bfloat16
    )
    total_new = jnp.sum(p_new.astype(jnp.float32), axis=-1)
    accum_new = jnp.einsum("ghqk,gkhd->ghqd", p_new, v_grp, preferred_element_type=jnp.float32)
    up_piece = lax.all_gather(up_weight, "req", axis=0, tiled=True)
    dense_piece = lax.all_gather(dense_weight, "req", axis=1, tiled=True)
    down_piece = lax.all_gather(down_weight, "req", axis=1, tiled=True)
    dense_piece = by_slot(dense_piece, split)
    down_piece = by_slot(down_piece, split)
    local_cache = cache[0]
    slots_here = local_cache.shape[0]
    slot_ids = me_kv * slots_here + jnp.arange(slots_here, dtype=jnp.int32)
    match = (page_table[None, :, :] == slot_ids[:, None, None]).astype(jnp.int32)
    owner_req = jnp.sum(
        match * jnp.arange(groups_here, dtype=jnp.int32)[None, :, None], axis=(1, 2)
    )
    owner_page = jnp.sum(
        match * jnp.arange(page_table.shape[1], dtype=jnp.int32)[None, None, :], axis=(1, 2)
    )
    page_pos = jnp.arange(PAGE, dtype=jnp.int32)
    reqs = jnp.arange(groups_here, dtype=jnp.int32)
    live = (owner_req[None, :, None] == reqs[:, None, None]) & (
        owner_page[None, :, None] * PAGE + page_pos[None, None, :] < cached_len[:, None, None]
    )
    live = live.astype(jnp.int32).reshape(groups_here, slots_here * PAGE, 1)
    accums, tops, totals = attend_pages(q_all, local_cache, live, split)
    tops = tops.reshape(HEADS, groups_here, span_rows)
    totals = totals.reshape(HEADS, groups_here, span_rows)
    top_new = jnp.transpose(top_new, (1, 0, 2))
    total_new = jnp.transpose(total_new, (1, 0, 2))
    accum_new = jnp.transpose(accum_new, (1, 0, 2, 3))
    own = lax.dynamic_slice_in_dim(tops, slot_me, heads_loc, 0)
    with_new = lax.dynamic_update_slice_in_dim(tops, jnp.maximum(own, top_new), slot_me, 0)
    largest = max_staged(with_new)
    factor = jnp.exp(tops - largest)
    tot_rows = (totals * factor).reshape(HEADS, groups_here, span_rows // HD, HD)
    packed = jnp.concatenate([accums * factor[..., None], tot_rows], axis=2)
    packed, up_piece, dense_piece, down_piece = lax.optimization_barrier(
        (packed, up_piece, dense_piece, down_piece)
    )
    summed = lax.psum_scatter(packed, "y", scatter_dimension=0, tiled=True)
    up_acc = jnp.dot(h2, up_piece, preferred_element_type=jnp.float32)
    hidden = jax.nn.gelu(up_acc, approximate=False).astype(jnp.bfloat16)
    mlp = jnp.dot(hidden, down_piece, preferred_element_type=jnp.float32)
    summed, mlp = lax.optimization_barrier((summed, mlp))
    for name in ("z", "xh"):
        summed = lax.psum_scatter(summed, name, scatter_dimension=0, tiled=True)
    sum_acc = summed[:, :, :span_rows]
    sum_tot = summed[:, :, span_rows:].reshape(heads_loc, groups_here, span_rows)
    own_largest = lax.dynamic_slice_in_dim(largest, slot_me, heads_loc, 0)
    fresh = jnp.exp(top_new - own_largest)
    numer = sum_acc + accum_new * fresh[..., None]
    denom = sum_tot + total_new * fresh
    att = (numer / denom[..., None]).astype(jnp.bfloat16)
    att = jnp.transpose(att, (1, 2, 0, 3)).reshape(rows, width_loc)
    value = jnp.dot(att, dense_piece, preferred_element_type=jnp.float32) + mlp
    summed = scatter_staged(value, 1)
    width_out = D // n_kv
    residual = lax.dynamic_slice_in_dim(x, me_kv * width_out, width_out, 1)
    return residual + summed


def solution(mesh):
    kv_split = (4, 2, 4)
    devices = mesh.devices.reshape((mesh.shape["req"],) + kv_split)
    torus = jax.sharding.Mesh(devices, ("req",) + KV)
    placed = (
        P("req", None),
        P(),
        P("req", None, KV),
        P(KV, "req"),
        P("req", KV),
        P(KV, "req"),
        P("req", KV, None, None, None, None),
        P("req"),
        P("req", None),
    )
    return jax.shard_map(
        layer, mesh=torus, in_specs=placed, out_specs=P("req", KV), check_vma=False
    )
```

```python
import jax
import jax.numpy as jnp
from jax import lax
from jax.sharding import PartitionSpec as P
from jax.experimental import pallas as pl

D = 4096
HEADS = 32
HD = 128
ROT = 32
PAGE = 128
KV = ("z", "xh", "y")


def head_slot(h, nz, nxh, ny):
    return (h % ny * nz + h // (nxh * ny)) * nxh + h // ny % nxh


def by_slot(w, split):
    nz, nxh, ny = split
    lead = w.shape[0]
    blocks = w.reshape(lead, nz, nxh, ny, w.shape[1] // (nz * nxh * ny))
    return jnp.transpose(blocks, (0, 3, 1, 2, 4)).reshape(w.shape)


def scatter_staged(x, dim):
    for name in ("y", ("z", "xh")):
        x = lax.psum_scatter(x, name, scatter_dimension=dim, tiled=True)
    return x


def gather_staged(x, dim):
    for name in ("y", ("z", "xh")):
        x = lax.all_gather(x, name, axis=dim, tiled=True)
    return x


def max_staged(x):
    for name in ("y", "xh", "z"):
        x = jnp.max(lax.all_gather(x, name, axis=0, tiled=False), axis=0)
    return x


def layer_norm(x, gain):
    mean = jnp.mean(x, axis=-1, keepdims=True)
    cent = x - mean
    var = jnp.mean(cent * cent, axis=-1, keepdims=True)
    return cent * lax.rsqrt(var + 1e-05) * gain


def rotate(t, pos):
    half = ROT // 2
    freq = 10000.0 ** (-(jnp.arange(half, dtype=jnp.float32) * 2.0 / ROT))
    angle = pos[:, None] * freq[None, :]
    cosine = jnp.cos(angle)[:, None, :]
    sine = jnp.sin(angle)[:, None, :]
    first = t[..., :half]
    second = t[..., half:ROT]
    return jnp.concatenate(
        [first * cosine - second * sine, second * cosine + first * sine, t[..., ROT:]], axis=-1
    )


def attend_kernel(q_ref, k_ref, v_ref, live_ref, acc_ref, top_ref, tot_ref):
    scale = 1.0 / HD**0.5
    slots = k_ref.shape[0]
    q = q_ref[...]
    k = k_ref[...].reshape(slots * PAGE, HD)
    v = v_ref[...].reshape(slots * PAGE, HD)
    scores = (
        lax.dot_general(k, q, (((1,), (1,)), ((), ())), preferred_element_type=jnp.float32)
        * scale
    )
    live = live_ref[...] > 0
    top = jnp.max(jnp.where(live, scores, -1e30), axis=0, keepdims=True)
    weights = jnp.where(live, jnp.exp(scores - top), 0.0).astype(jnp.bfloat16)
    tot_ref[...] = jnp.sum(weights.astype(jnp.float32), axis=0, keepdims=True)
    top_ref[...] = top
    acc_ref[...] = lax.dot_general(
        weights, v, (((0,), (0,)), ((), ())), preferred_element_type=jnp.float32
    )


def attend_pages(q_all, local_cache, live, split):
    groups, span = live.shape[0], q_all.shape[0] // live.shape[0]
    slots = local_cache.shape[0]
    heads = local_cache.shape[2]
    page_spec = lambda kv: pl.BlockSpec(
        (slots, None, None, PAGE, HD), lambda g, h: (0, kv, h, 0, 0)
    )
    row_spec = pl.BlockSpec((None, None, 1, span), lambda g, h: (head_slot(h, *split), g, 0, 0))
    return pl.pallas_call(
        attend_kernel,
        grid=(groups, heads),
        in_specs=[
            pl.BlockSpec((span, HD), lambda g, h: (g, h)),
            page_spec(0),
            page_spec(1),
            pl.BlockSpec((None, slots * PAGE, 1), lambda g, h: (g, 0, 0)),
        ],
        out_specs=[
            pl.BlockSpec((None, None, span, HD), lambda g, h: (head_slot(h, *split), g, 0, 0)),
            row_spec,
            row_spec,
        ],
        out_shape=[
            jax.ShapeDtypeStruct((heads, groups, span, HD), jnp.float32),
            jax.ShapeDtypeStruct((heads, groups, 1, span), jnp.float32),
            jax.ShapeDtypeStruct((heads, groups, 1, span), jnp.float32),
        ],
        cost_estimate=pl.CostEstimate(
            flops=4 * groups * heads * span * slots * PAGE * HD,
            transcendentals=groups * heads * span * slots * PAGE,
            bytes_accessed=groups * local_cache.size * 2 + q_all.size * 2
            + groups * heads * span * HD * 4,
        ),
    )(q_all, local_cache, local_cache, live)


def layer(
    hidden_in,
    ln_gains,
    qkv_weight,
    dense_weight,
    up_weight,
    down_weight,
    cache,
    cached_len,
    page_table,
):
    split = tuple(lax.axis_size(name) for name in KV)
    n_kv = split[0] * split[1] * split[2]
    me_kv = lax.axis_index(KV)
    slot_me = head_slot(me_kv, *split)
    rows = hidden_in.shape[0]
    groups_here = cached_len.shape[0]
    span_rows = rows // groups_here
    width_loc = qkv_weight.shape[2]
    heads_loc = width_loc // HD
    scale = 1.0 / HD**0.5
    x = hidden_in.astype(jnp.float32)
    h1 = layer_norm(x, ln_gains[0]).astype(jnp.bfloat16)
    h2 = layer_norm(x, ln_gains[1]).astype(jnp.bfloat16)
    q_piece = lax.all_gather(qkv_weight[:, 0], "req", axis=0, tiled=True)
    q_acc = jnp.dot(h1, q_piece, preferred_element_type=jnp.float32)
    offsets = jnp.arange(span_rows, dtype=jnp.int32)
    pos = (cached_len[:, None] + offsets[None, :]).reshape(rows).astype(jnp.float32)
    query = rotate(q_acc.reshape(rows, heads_loc, HD), pos).astype(jnp.bfloat16)
    q_all = gather_staged(query.reshape(rows, width_loc), 1)
    kv_weight, up_weight, dense_weight, down_weight, q_all = lax.optimization_barrier(
        (qkv_weight[:, 1:], up_weight, dense_weight, down_weight, q_all)
    )
    kv_piece = lax.all_gather(kv_weight, "req", axis=0, tiled=True)
    count = kv_piece.shape[0]
    kv_acc = jnp.dot(
        h1, kv_piece.reshape(count, 2 * width_loc), preferred_element_type=jnp.float32
    ).reshape(rows, 2, heads_loc, HD)
    key_new = rotate(kv_acc[:, 0], pos).astype(jnp.bfloat16)
    value_new = kv_acc[:, 1].astype(jnp.bfloat16)
    q_grp = query.reshape(groups_here, span_rows, heads_loc, HD)
    k_grp = key_new.reshape(groups_here, span_rows, heads_loc, HD)
    v_grp = value_new.reshape(groups_here, span_rows, heads_loc, HD)
    causal = offsets[None, :] <= offsets[:, None]
    s_new = jnp.einsum("gqhd,gkhd->ghqk", q_grp, k_grp, preferred_element_type=jnp.float32) * scale
    s_new = jnp.where(causal[None, None], s_new, -1e30)
    top_new = jnp.max(s_new, axis=-1)
    p_new = jnp.where(causal[None, None], jnp.exp(s_new - top_new[..., None]), 0.0).astype(
        jnp.bfloat16
    )
    total_new = jnp.sum(p_new.astype(jnp.float32), axis=-1)
    accum_new = jnp.einsum("ghqk,gkhd->ghqd", p_new, v_grp, preferred_element_type=jnp.float32)
    up_piece = lax.all_gather(up_weight, "req", axis=0, tiled=True)
    dense_piece = lax.all_gather(dense_weight, "req", axis=1, tiled=True)
    down_piece = lax.all_gather(down_weight, "req", axis=1, tiled=True)
    dense_piece = by_slot(dense_piece, split)
    down_piece = by_slot(down_piece, split)
    local_cache = cache[0]
    slots_here = local_cache.shape[0]
    slot_ids = me_kv * slots_here + jnp.arange(slots_here, dtype=jnp.int32)
    match = (page_table[None, :, :] == slot_ids[:, None, None]).astype(jnp.int32)
    owner_req = jnp.sum(
        match * jnp.arange(groups_here, dtype=jnp.int32)[None, :, None], axis=(1, 2)
    )
    owner_page = jnp.sum(
        match * jnp.arange(page_table.shape[1], dtype=jnp.int32)[None, None, :], axis=(1, 2)
    )
    page_pos = jnp.arange(PAGE, dtype=jnp.int32)
    reqs = jnp.arange(groups_here, dtype=jnp.int32)
    live = (owner_req[None, :, None] == reqs[:, None, None]) & (
        owner_page[None, :, None] * PAGE + page_pos[None, None, :] < cached_len[:, None, None]
    )
    live = live.astype(jnp.int32).reshape(groups_here, slots_here * PAGE, 1)
    accums, tops, totals = attend_pages(q_all, local_cache, live, split)
    tops = tops.reshape(HEADS, groups_here, span_rows)
    totals = totals.reshape(HEADS, groups_here, span_rows)
    top_new = jnp.transpose(top_new, (1, 0, 2))
    total_new = jnp.transpose(total_new, (1, 0, 2))
    accum_new = jnp.transpose(accum_new, (1, 0, 2, 3))
    own = lax.dynamic_slice_in_dim(tops, slot_me, heads_loc, 0)
    with_new = lax.dynamic_update_slice_in_dim(tops, jnp.maximum(own, top_new), slot_me, 0)
    largest = max_staged(with_new)
    factor = jnp.exp(tops - largest)
    tot_rows = (totals * factor).reshape(HEADS, groups_here, span_rows // HD, HD)
    packed = jnp.concatenate([accums * factor[..., None], tot_rows], axis=2)
    packed, up_piece, dense_piece, down_piece = lax.optimization_barrier(
        (packed, up_piece, dense_piece, down_piece)
    )
    summed = lax.psum_scatter(packed, "y", scatter_dimension=0, tiled=True)
    up_acc = jnp.dot(h2, up_piece, preferred_element_type=jnp.float32)
    hidden = jax.nn.gelu(up_acc, approximate=False).astype(jnp.bfloat16)
    mlp = jnp.dot(hidden, down_piece, preferred_element_type=jnp.float32)
    summed, mlp = lax.optimization_barrier((summed, mlp))
    summed = lax.psum_scatter(summed, ("z", "xh"), scatter_dimension=0, tiled=True)
    sum_acc = summed[:, :, :span_rows]
    sum_tot = summed[:, :, span_rows:].reshape(heads_loc, groups_here, span_rows)
    own_largest = lax.dynamic_slice_in_dim(largest, slot_me, heads_loc, 0)
    fresh = jnp.exp(top_new - own_largest)
    numer = sum_acc + accum_new * fresh[..., None]
    denom = sum_tot + total_new * fresh
    att = (numer / denom[..., None]).astype(jnp.bfloat16)
    att = jnp.transpose(att, (1, 2, 0, 3)).reshape(rows, width_loc)
    value = jnp.dot(att, dense_piece, preferred_element_type=jnp.float32) + mlp
    summed = scatter_staged(value, 1)
    width_out = D // n_kv
    residual = lax.dynamic_slice_in_dim(x, me_kv * width_out, width_out, 1)
    return residual + summed


def solution(mesh):
    kv_split = (4, 2, 4)
    devices = mesh.devices.reshape((mesh.shape["req"],) + kv_split)
    torus = jax.sharding.Mesh(devices, ("req",) + KV)
    placed = (
        P("req", None),
        P(),
        P("req", None, KV),
        P(KV, "req"),
        P("req", KV),
        P(KV, "req"),
        P("req", KV, None, None, None, None),
        P("req"),
        P("req", None),
    )
    return jax.shard_map(
        layer, mesh=torus, in_specs=placed, out_specs=P("req", KV), check_vma=False
    )
```

```python
import jax
import jax.numpy as jnp
from jax import lax
from jax.sharding import PartitionSpec as P
from jax.experimental import pallas as pl

D = 4096
HEADS = 32
HD = 128
ROT = 32
PAGE = 128
KV = ("z", "xh", "y")


def head_slot(h, nz, nxh, ny):
    return (h % ny * nz + h // (nxh * ny)) * nxh + h // ny % nxh


def by_slot(w, split):
    nz, nxh, ny = split
    lead = w.shape[0]
    blocks = w.reshape(lead, nz, nxh, ny, w.shape[1] // (nz * nxh * ny))
    return jnp.transpose(blocks, (0, 3, 1, 2, 4)).reshape(w.shape)


def gather_req_ring(w):
    n = lax.axis_size("req")
    me = lax.axis_index("req")
    parts = [w] + [
        lax.ppermute(w, "req", [(i, (i + s) % n) for i in range(n)]) for s in range(1, n)
    ]
    ordered = jnp.take(jnp.stack(parts), (me - jnp.arange(n)) % n, axis=0)
    return ordered.reshape((n * w.shape[0],) + w.shape[1:])


def scatter_staged(x, dim):
    for name in ("y", "z", "xh"):
        x = lax.psum_scatter(x, name, scatter_dimension=dim, tiled=True)
    return x


def gather_staged(x, dim):
    for name in ("y", "xh", "z"):
        x = lax.all_gather(x, name, axis=dim, tiled=True)
    return x


def max_staged(x):
    for name in ("y", "xh", "z"):
        x = jnp.max(lax.all_gather(x, name, axis=0, tiled=False), axis=0)
    return x


def layer_norm(x, gain):
    mean = jnp.mean(x, axis=-1, keepdims=True)
    cent = x - mean
    var = jnp.mean(cent * cent, axis=-1, keepdims=True)
    return cent * lax.rsqrt(var + 1e-05) * gain


def rotate(t, pos):
    half = ROT // 2
    freq = 10000.0 ** (-(jnp.arange(half, dtype=jnp.float32) * 2.0 / ROT))
    angle = pos[:, None] * freq[None, :]
    cosine = jnp.cos(angle)[:, None, :]
    sine = jnp.sin(angle)[:, None, :]
    first = t[..., :half]
    second = t[..., half:ROT]
    return jnp.concatenate(
        [first * cosine - second * sine, second * cosine + first * sine, t[..., ROT:]], axis=-1
    )


def attend_kernel(q_ref, k_ref, v_ref, live_ref, acc_ref, top_ref, tot_ref):
    scale = 1.0 / HD**0.5
    slots = k_ref.shape[0]
    q = q_ref[...]
    k = k_ref[...].reshape(slots * PAGE, HD)
    v = v_ref[...].reshape(slots * PAGE, HD)
    scores = (
        lax.dot_general(k, q, (((1,), (1,)), ((), ())), preferred_element_type=jnp.float32)
        * scale
    )
    live = live_ref[...] > 0
    top = jnp.max(jnp.where(live, scores, -1e30), axis=0, keepdims=True)
    weights = jnp.where(live, jnp.exp(scores - top), 0.0).astype(jnp.bfloat16)
    tot_ref[...] = jnp.sum(weights.astype(jnp.float32), axis=0, keepdims=True)
    top_ref[...] = top
    acc_ref[...] = lax.dot_general(
        weights, v, (((0,), (0,)), ((), ())), preferred_element_type=jnp.float32
    )


def attend_pages(q_all, local_cache, live, split):
    groups, span = live.shape[0], q_all.shape[0] // live.shape[0]
    slots = local_cache.shape[0]
    heads = local_cache.shape[2]
    page_spec = lambda kv: pl.BlockSpec(
        (slots, None, None, PAGE, HD), lambda g, h: (0, kv, h, 0, 0)
    )
    row_spec = pl.BlockSpec((None, None, 1, span), lambda g, h: (head_slot(h, *split), g, 0, 0))
    return pl.pallas_call(
        attend_kernel,
        grid=(groups, heads),
        in_specs=[
            pl.BlockSpec((span, HD), lambda g, h: (g, h)),
            page_spec(0),
            page_spec(1),
            pl.BlockSpec((None, slots * PAGE, 1), lambda g, h: (g, 0, 0)),
        ],
        out_specs=[
            pl.BlockSpec((None, None, span, HD), lambda g, h: (head_slot(h, *split), g, 0, 0)),
            row_spec,
            row_spec,
        ],
        out_shape=[
            jax.ShapeDtypeStruct((heads, groups, span, HD), jnp.float32),
            jax.ShapeDtypeStruct((heads, groups, 1, span), jnp.float32),
            jax.ShapeDtypeStruct((heads, groups, 1, span), jnp.float32),
        ],
        cost_estimate=pl.CostEstimate(
            flops=4 * groups * heads * span * slots * PAGE * HD,
            transcendentals=groups * heads * span * slots * PAGE,
            bytes_accessed=groups * local_cache.size * 2 + q_all.size * 2
            + groups * heads * span * HD * 4,
        ),
    )(q_all, local_cache, local_cache, live)


def layer(
    hidden_in,
    ln_gains,
    qkv_weight,
    dense_weight,
    up_weight,
    down_weight,
    cache,
    cached_len,
    page_table,
):
    split = tuple(lax.axis_size(name) for name in KV)
    n_kv = split[0] * split[1] * split[2]
    me_kv = lax.axis_index(KV)
    slot_me = head_slot(me_kv, *split)
    rows = hidden_in.shape[0]
    groups_here = cached_len.shape[0]
    span_rows = rows // groups_here
    width_loc = qkv_weight.shape[2]
    heads_loc = width_loc // HD
    scale = 1.0 / HD**0.5
    x = hidden_in.astype(jnp.float32)
    h1 = layer_norm(x, ln_gains[0]).astype(jnp.bfloat16)
    h2 = layer_norm(x, ln_gains[1]).astype(jnp.bfloat16)
    q_piece = lax.all_gather(qkv_weight[:, 0], "req", axis=0, tiled=True)
    q_acc = jnp.dot(h1, q_piece, preferred_element_type=jnp.float32)
    offsets = jnp.arange(span_rows, dtype=jnp.int32)
    pos = (cached_len[:, None] + offsets[None, :]).reshape(rows).astype(jnp.float32)
    query = rotate(q_acc.reshape(rows, heads_loc, HD), pos).astype(jnp.bfloat16)
    q_all = gather_staged(query.reshape(rows, width_loc), 1)
    kv_weight, up_weight, dense_weight, down_weight, q_all = lax.optimization_barrier(
        (qkv_weight[:, 1:], up_weight, dense_weight, down_weight, q_all)
    )
    kv_piece = lax.all_gather(kv_weight, "req", axis=0, tiled=True)
    count = kv_piece.shape[0]
    kv_acc = jnp.dot(
        h1, kv_piece.reshape(count, 2 * width_loc), preferred_element_type=jnp.float32
    ).reshape(rows, 2, heads_loc, HD)
    key_new = rotate(kv_acc[:, 0], pos).astype(jnp.bfloat16)
    value_new = kv_acc[:, 1].astype(jnp.bfloat16)
    q_grp = query.reshape(groups_here, span_rows, heads_loc, HD)
    k_grp = key_new.reshape(groups_here, span_rows, heads_loc, HD)
    v_grp = value_new.reshape(groups_here, span_rows, heads_loc, HD)
    causal = offsets[None, :] <= offsets[:, None]
    s_new = jnp.einsum("gqhd,gkhd->ghqk", q_grp, k_grp, preferred_element_type=jnp.float32) * scale
    s_new = jnp.where(causal[None, None], s_new, -1e30)
    top_new = jnp.max(s_new, axis=-1)
    p_new = jnp.where(causal[None, None], jnp.exp(s_new - top_new[..., None]), 0.0).astype(
        jnp.bfloat16
    )
    total_new = jnp.sum(p_new.astype(jnp.float32), axis=-1)
    accum_new = jnp.einsum("ghqk,gkhd->ghqd", p_new, v_grp, preferred_element_type=jnp.float32)
    up_piece = gather_req_ring(up_weight)
    dense_piece = lax.all_gather(dense_weight, "req", axis=1, tiled=True)
    down_piece = lax.all_gather(down_weight, "req", axis=1, tiled=True)
    dense_piece = by_slot(dense_piece, split)
    down_piece = by_slot(down_piece, split)
    local_cache = cache[0]
    slots_here = local_cache.shape[0]
    slot_ids = me_kv * slots_here + jnp.arange(slots_here, dtype=jnp.int32)
    match = (page_table[None, :, :] == slot_ids[:, None, None]).astype(jnp.int32)
    owner_req = jnp.sum(
        match * jnp.arange(groups_here, dtype=jnp.int32)[None, :, None], axis=(1, 2)
    )
    owner_page = jnp.sum(
        match * jnp.arange(page_table.shape[1], dtype=jnp.int32)[None, None, :], axis=(1, 2)
    )
    page_pos = jnp.arange(PAGE, dtype=jnp.int32)
    reqs = jnp.arange(groups_here, dtype=jnp.int32)
    live = (owner_req[None, :, None] == reqs[:, None, None]) & (
        owner_page[None, :, None] * PAGE + page_pos[None, None, :] < cached_len[:, None, None]
    )
    live = live.astype(jnp.int32).reshape(groups_here, slots_here * PAGE, 1)
    accums, tops, totals = attend_pages(q_all, local_cache, live, split)
    tops = tops.reshape(HEADS, groups_here, span_rows)
    totals = totals.reshape(HEADS, groups_here, span_rows)
    top_new = jnp.transpose(top_new, (1, 0, 2))
    total_new = jnp.transpose(total_new, (1, 0, 2))
    accum_new = jnp.transpose(accum_new, (1, 0, 2, 3))
    own = lax.dynamic_slice_in_dim(tops, slot_me, heads_loc, 0)
    with_new = lax.dynamic_update_slice_in_dim(tops, jnp.maximum(own, top_new), slot_me, 0)
    largest = max_staged(with_new)
    factor = jnp.exp(tops - largest)
    tot_rows = (totals * factor).reshape(HEADS, groups_here, span_rows // HD, HD)
    packed = jnp.concatenate([accums * factor[..., None], tot_rows], axis=2)
    packed, up_piece, dense_piece, down_piece = lax.optimization_barrier(
        (packed, up_piece, dense_piece, down_piece)
    )
    summed = lax.psum_scatter(packed, "y", scatter_dimension=0, tiled=True)
    up_acc = jnp.dot(h2, up_piece, preferred_element_type=jnp.float32)
    hidden = jax.nn.gelu(up_acc, approximate=False).astype(jnp.bfloat16)
    mlp = jnp.dot(hidden, down_piece, preferred_element_type=jnp.float32)
    summed, mlp = lax.optimization_barrier((summed, mlp))
    for name in ("z", "xh"):
        summed = lax.psum_scatter(summed, name, scatter_dimension=0, tiled=True)
    sum_acc = summed[:, :, :span_rows]
    sum_tot = summed[:, :, span_rows:].reshape(heads_loc, groups_here, span_rows)
    own_largest = lax.dynamic_slice_in_dim(largest, slot_me, heads_loc, 0)
    fresh = jnp.exp(top_new - own_largest)
    numer = sum_acc + accum_new * fresh[..., None]
    denom = sum_tot + total_new * fresh
    att = (numer / denom[..., None]).astype(jnp.bfloat16)
    att = jnp.transpose(att, (1, 2, 0, 3)).reshape(rows, width_loc)
    value = jnp.dot(att, dense_piece, preferred_element_type=jnp.float32) + mlp
    summed = scatter_staged(value, 1)
    width_out = D // n_kv
    residual = lax.dynamic_slice_in_dim(x, me_kv * width_out, width_out, 1)
    return residual + summed


def solution(mesh):
    kv_split = (4, 2, 4)
    devices = mesh.devices.reshape((mesh.shape["req"],) + kv_split)
    torus = jax.sharding.Mesh(devices, ("req",) + KV)
    placed = (
        P("req", None),
        P(),
        P("req", None, KV),
        P(KV, "req"),
        P("req", KV),
        P(KV, "req"),
        P("req", KV, None, None, None, None),
        P("req"),
        P("req", None),
    )
    return jax.shard_map(
        layer, mesh=torus, in_specs=placed, out_specs=P("req", KV), check_vma=False
    )
```

```python
import jax
import jax.numpy as jnp
from jax import lax
from jax.sharding import PartitionSpec as P
from jax.experimental import pallas as pl

D = 4096
HEADS = 32
HD = 128
ROT = 32
PAGE = 128
KV = ("z", "xh", "y")


def head_slot(h, nz, nxh, ny):
    return (h % ny * nz + h // (nxh * ny)) * nxh + h // ny % nxh


def by_slot(w, split):
    nz, nxh, ny = split
    lead = w.shape[0]
    blocks = w.reshape(lead, nz, nxh, ny, w.shape[1] // (nz * nxh * ny))
    return jnp.transpose(blocks, (0, 3, 1, 2, 4)).reshape(w.shape)


def gather_req_ring(w):
    n = lax.axis_size("req")
    me = lax.axis_index("req")
    parts = [w] + [
        lax.ppermute(w, "req", [(i, (i + s) % n) for i in range(n)]) for s in range(1, n)
    ]
    ordered = jnp.take(jnp.stack(parts), (me - jnp.arange(n)) % n, axis=0)
    return ordered.reshape((n * w.shape[0],) + w.shape[1:])


def scatter_staged(x, dim):
    for name in ("y", "z", "xh"):
        x = lax.psum_scatter(x, name, scatter_dimension=dim, tiled=True)
    return x


def gather_staged(x, dim):
    for name in ("y", "xh", "z"):
        x = lax.all_gather(x, name, axis=dim, tiled=True)
    return x


def max_staged(x):
    for name in (("xh", "y"), "z"):
        x = jnp.max(lax.all_gather(x, name, axis=0, tiled=False), axis=0)
    return x


def layer_norm(x, gain):
    mean = jnp.mean(x, axis=-1, keepdims=True)
    cent = x - mean
    var = jnp.mean(cent * cent, axis=-1, keepdims=True)
    return cent * lax.rsqrt(var + 1e-05) * gain


def rotate(t, pos):
    half = ROT // 2
    freq = 10000.0 ** (-(jnp.arange(half, dtype=jnp.float32) * 2.0 / ROT))
    angle = pos[:, None] * freq[None, :]
    cosine = jnp.cos(angle)[:, None, :]
    sine = jnp.sin(angle)[:, None, :]
    first = t[..., :half]
    second = t[..., half:ROT]
    return jnp.concatenate(
        [first * cosine - second * sine, second * cosine + first * sine, t[..., ROT:]], axis=-1
    )


def attend_kernel(q_ref, k_ref, v_ref, live_ref, acc_ref, top_ref, tot_ref):
    scale = 1.0 / HD**0.5
    slots = k_ref.shape[0]
    q = q_ref[...]
    k = k_ref[...].reshape(slots * PAGE, HD)
    v = v_ref[...].reshape(slots * PAGE, HD)
    scores = (
        lax.dot_general(k, q, (((1,), (1,)), ((), ())), preferred_element_type=jnp.float32)
        * scale
    )
    live = live_ref[...] > 0
    top = jnp.max(jnp.where(live, scores, -1e30), axis=0, keepdims=True)
    weights = jnp.where(live, jnp.exp(scores - top), 0.0).astype(jnp.bfloat16)
    tot_ref[...] = jnp.sum(weights.astype(jnp.float32), axis=0, keepdims=True)
    top_ref[...] = top
    acc_ref[...] = lax.dot_general(
        weights, v, (((0,), (0,)), ((), ())), preferred_element_type=jnp.float32
    )


def attend_pages(q_all, local_cache, live, split):
    groups, span = live.shape[0], q_all.shape[0] // live.shape[0]
    slots = local_cache.shape[0]
    heads = local_cache.shape[2]
    page_spec = lambda kv: pl.BlockSpec(
        (slots, None, None, PAGE, HD), lambda g, h: (0, kv, h, 0, 0)
    )
    row_spec = pl.BlockSpec((None, None, 1, span), lambda g, h: (head_slot(h, *split), g, 0, 0))
    return pl.pallas_call(
        attend_kernel,
        grid=(groups, heads),
        in_specs=[
            pl.BlockSpec((span, HD), lambda g, h: (g, h)),
            page_spec(0),
            page_spec(1),
            pl.BlockSpec((None, slots * PAGE, 1), lambda g, h: (g, 0, 0)),
        ],
        out_specs=[
            pl.BlockSpec((None, None, span, HD), lambda g, h: (head_slot(h, *split), g, 0, 0)),
            row_spec,
            row_spec,
        ],
        out_shape=[
            jax.ShapeDtypeStruct((heads, groups, span, HD), jnp.float32),
            jax.ShapeDtypeStruct((heads, groups, 1, span), jnp.float32),
            jax.ShapeDtypeStruct((heads, groups, 1, span), jnp.float32),
        ],
        cost_estimate=pl.CostEstimate(
            flops=4 * groups * heads * span * slots * PAGE * HD,
            transcendentals=groups * heads * span * slots * PAGE,
            bytes_accessed=groups * local_cache.size * 2 + q_all.size * 2
            + groups * heads * span * HD * 4,
        ),
    )(q_all, local_cache, local_cache, live)


def layer(
    hidden_in,
    ln_gains,
    qkv_weight,
    dense_weight,
    up_weight,
    down_weight,
    cache,
    cached_len,
    page_table,
):
    split = tuple(lax.axis_size(name) for name in KV)
    n_kv = split[0] * split[1] * split[2]
    me_kv = lax.axis_index(KV)
    slot_me = head_slot(me_kv, *split)
    rows = hidden_in.shape[0]
    groups_here = cached_len.shape[0]
    span_rows = rows // groups_here
    width_loc = qkv_weight.shape[2]
    heads_loc = width_loc // HD
    scale = 1.0 / HD**0.5
    x = hidden_in.astype(jnp.float32)
    h1 = layer_norm(x, ln_gains[0]).astype(jnp.bfloat16)
    h2 = layer_norm(x, ln_gains[1]).astype(jnp.bfloat16)
    q_piece = lax.all_gather(qkv_weight[:, 0], "req", axis=0, tiled=True)
    q_acc = jnp.dot(h1, q_piece, preferred_element_type=jnp.float32)
    offsets = jnp.arange(span_rows, dtype=jnp.int32)
    pos = (cached_len[:, None] + offsets[None, :]).reshape(rows).astype(jnp.float32)
    query = rotate(q_acc.reshape(rows, heads_loc, HD), pos).astype(jnp.bfloat16)
    q_all = gather_staged(query.reshape(rows, width_loc), 1)
    kv_weight, up_weight, dense_weight, down_weight, q_all = lax.optimization_barrier(
        (qkv_weight[:, 1:], up_weight, dense_weight, down_weight, q_all)
    )
    kv_piece = lax.all_gather(kv_weight, "req", axis=0, tiled=True)
    count = kv_piece.shape[0]
    kv_acc = jnp.dot(
        h1, kv_piece.reshape(count, 2 * width_loc), preferred_element_type=jnp.float32
    ).reshape(rows, 2, heads_loc, HD)
    key_new = rotate(kv_acc[:, 0], pos).astype(jnp.bfloat16)
    value_new = kv_acc[:, 1].astype(jnp.bfloat16)
    q_grp = query.reshape(groups_here, span_rows, heads_loc, HD)
    k_grp = key_new.reshape(groups_here, span_rows, heads_loc, HD)
    v_grp = value_new.reshape(groups_here, span_rows, heads_loc, HD)
    causal = offsets[None, :] <= offsets[:, None]
    s_new = jnp.einsum("gqhd,gkhd->ghqk", q_grp, k_grp, preferred_element_type=jnp.float32) * scale
    s_new = jnp.where(causal[None, None], s_new, -1e30)
    top_new = jnp.max(s_new, axis=-1)
    p_new = jnp.where(causal[None, None], jnp.exp(s_new - top_new[..., None]), 0.0).astype(
        jnp.bfloat16
    )
    total_new = jnp.sum(p_new.astype(jnp.float32), axis=-1)
    accum_new = jnp.einsum("ghqk,gkhd->ghqd", p_new, v_grp, preferred_element_type=jnp.float32)
    up_piece = gather_req_ring(up_weight)
    dense_piece = lax.all_gather(dense_weight, "req", axis=1, tiled=True)
    down_piece = lax.all_gather(down_weight, "req", axis=1, tiled=True)
    dense_piece = by_slot(dense_piece, split)
    down_piece = by_slot(down_piece, split)
    local_cache = cache[0]
    slots_here = local_cache.shape[0]
    slot_ids = me_kv * slots_here + jnp.arange(slots_here, dtype=jnp.int32)
    match = (page_table[None, :, :] == slot_ids[:, None, None]).astype(jnp.int32)
    owner_req = jnp.sum(
        match * jnp.arange(groups_here, dtype=jnp.int32)[None, :, None], axis=(1, 2)
    )
    owner_page = jnp.sum(
        match * jnp.arange(page_table.shape[1], dtype=jnp.int32)[None, None, :], axis=(1, 2)
    )
    page_pos = jnp.arange(PAGE, dtype=jnp.int32)
    reqs = jnp.arange(groups_here, dtype=jnp.int32)
    live = (owner_req[None, :, None] == reqs[:, None, None]) & (
        owner_page[None, :, None] * PAGE + page_pos[None, None, :] < cached_len[:, None, None]
    )
    live = live.astype(jnp.int32).reshape(groups_here, slots_here * PAGE, 1)
    accums, tops, totals = attend_pages(q_all, local_cache, live, split)
    tops = tops.reshape(HEADS, groups_here, span_rows)
    totals = totals.reshape(HEADS, groups_here, span_rows)
    top_new = jnp.transpose(top_new, (1, 0, 2))
    total_new = jnp.transpose(total_new, (1, 0, 2))
    accum_new = jnp.transpose(accum_new, (1, 0, 2, 3))
    own = lax.dynamic_slice_in_dim(tops, slot_me, heads_loc, 0)
    with_new = lax.dynamic_update_slice_in_dim(tops, jnp.maximum(own, top_new), slot_me, 0)
    largest = max_staged(with_new)
    factor = jnp.exp(tops - largest)
    tot_rows = (totals * factor).reshape(HEADS, groups_here, span_rows // HD, HD)
    packed = jnp.concatenate([accums * factor[..., None], tot_rows], axis=2)
    packed, dense_piece, down_piece = lax.optimization_barrier((packed, dense_piece, down_piece))
    summed = lax.psum_scatter(packed, "y", scatter_dimension=0, tiled=True)
    up_acc = jnp.dot(h2, up_piece, preferred_element_type=jnp.float32)
    hidden = jax.nn.gelu(up_acc, approximate=False).astype(jnp.bfloat16)
    mlp = jnp.dot(hidden, down_piece, preferred_element_type=jnp.float32)
    summed, mlp = lax.optimization_barrier((summed, mlp))
    for name in ("z", "xh"):
        summed = lax.psum_scatter(summed, name, scatter_dimension=0, tiled=True)
    sum_acc = summed[:, :, :span_rows]
    sum_tot = summed[:, :, span_rows:].reshape(heads_loc, groups_here, span_rows)
    own_largest = lax.dynamic_slice_in_dim(largest, slot_me, heads_loc, 0)
    fresh = jnp.exp(top_new - own_largest)
    numer = sum_acc + accum_new * fresh[..., None]
    denom = sum_tot + total_new * fresh
    att = (numer / denom[..., None]).astype(jnp.bfloat16)
    att = jnp.transpose(att, (1, 2, 0, 3)).reshape(rows, width_loc)
    value = jnp.dot(att, dense_piece, preferred_element_type=jnp.float32) + mlp
    summed = scatter_staged(value, 1)
    width_out = D // n_kv
    residual = lax.dynamic_slice_in_dim(x, me_kv * width_out, width_out, 1)
    return residual + summed


def solution(mesh):
    kv_split = (4, 2, 4)
    devices = mesh.devices.reshape((mesh.shape["req"],) + kv_split)
    torus = jax.sharding.Mesh(devices, ("req",) + KV)
    placed = (
        P("req", None),
        P(),
        P("req", None, KV),
        P(KV, "req"),
        P("req", KV),
        P(KV, "req"),
        P("req", KV, None, None, None, None),
        P("req"),
        P("req", None),
    )
    return jax.shard_map(
        layer, mesh=torus, in_specs=placed, out_specs=P("req", KV), check_vma=False
    )
```
